128 devices in a mesh: pts: 8 (over y, core), cen: 16 (over x, z).
Axes of the slice: x: 4, y: 4, z: 4, core: 2. Of those that a mesh axis runs over, the one named last changes fastest.
Arguments:
- points: bfloat16 [16384, 768], P('pts', 'cen'), may hold values from -6 to 6
- centroids: bfloat16 [32768, 768], P('cen'), may hold values from -6 to 6
Outputs:
- new_centroids: float32 [32768, 768], P('cen', 'pts')
- masses: float32 [32768], P('cen')
The draws below stay inside these ranges and needn't reach their ends.
All inputs are finite; a program needn't handle non-finite values.
Results may differ from the reference program's by a relative error of at most 0.00089.
Values may be sent and summed in bfloat16 or wider, within the bound.
No kernel may reach another device: no remote copies, remote signals or barrier semaphores. Data moves between devices by JAX's collectives and lax.ppermute only.
A program may use at most 128 MiB of HBM per device.

```python
import jax
import jax.numpy as jnp
from jax import lax

D = 768
ITERS = 3
POINTS = 16384
CENTROIDS = 32768


def cluster_centres(key):
    clusters = max(8, CENTROIDS // 128)
    centres = jnp.clip(jax.random.normal(jax.random.fold_in(key, 7), (clusters, D), jnp.float32), -4.0, 4.0)
    return (clusters, centres)


def draw_points(key, part):
    clusters, centres = cluster_centres(key)
    root_key = jax.random.fold_in(key, 19)
    subkeys = jax.random.split(root_key, 3)
    ticket = jax.random.randint(subkeys[0], (POINTS,), 0, 4096, jnp.int32)
    labels = ((ticket + ticket * ticket // 4096) * clusters // 8192).astype(jnp.int32)
    spread_draw = jax.random.uniform(subkeys[1], (POINTS, 1), jnp.float32)
    tightness = 0.3 + 0.5 * spread_draw
    jitter = jnp.clip(jax.random.normal(subkeys[2], (POINTS, D), jnp.float32), -4.0, 4.0)
    values = tightness * centres[labels] + jnp.sqrt(1.0 - tightness * tightness) * jitter
    return values.astype(jnp.bfloat16)


def draw_centroids(key, part):
    clusters, centres = cluster_centres(key)
    root_key = jax.random.fold_in(key, 23)
    subkeys = jax.random.split(root_key, 3)
    labels = jax.random.randint(subkeys[0], (CENTROIDS,), 0, clusters, jnp.int32)
    spread_draw = jax.random.uniform(subkeys[1], (CENTROIDS, 1), jnp.float32)
    tightness = 0.5 + 0.35 * spread_draw
    jitter = jnp.clip(jax.random.normal(subkeys[2], (CENTROIDS, D), jnp.float32), -4.0, 4.0)
    values = tightness * centres[labels] + jnp.sqrt(1.0 - tightness * tightness) * jitter
    return values.astype(jnp.bfloat16)


def setup_inputs(seed: int = 0) -> dict:
    arg_keys = jax.random.split(jax.random.key(seed), 3)
    return {
        "points": draw_points(jax.random.fold_in(arg_keys[2], 71), 0),
        "centroids": draw_centroids(jax.random.fold_in(arg_keys[2], 71), 0),
    }


temper = 0.05

def unit_rows(values):
    wide = values.astype(jnp.float32)
    return (wide * lax.rsqrt(lax.optimization_barrier(jnp.mean(wide * wide, axis=1, keepdims=True)) + 1e-06)).astype(jnp.bfloat16)

def reference(points, centroids):
    unit_points = unit_rows(points)
    unit_centroids = unit_rows(centroids)
    scores = jnp.dot(unit_points, unit_centroids.T, preferred_element_type=jnp.float32)
    kernel = jnp.exp(scores / (D * temper))
    count_pts = kernel.shape[0]
    count_cen = kernel.shape[1]
    balance = count_pts / count_cen
    row_scale = jnp.ones((count_pts,), jnp.float32)
    col_scale = jnp.ones((count_cen,), jnp.float32)
    for sweep in range(ITERS):
        col_scale = balance / lax.optimization_barrier(jnp.sum(kernel * row_scale[:, None], axis=0))
        row_scale = 1.0 / lax.optimization_barrier(jnp.sum(kernel * col_scale[None, :], axis=1))
    weights = row_scale[:, None] * kernel * col_scale[None, :]
    moved = lax.dot_general(weights, points.astype(jnp.float32), (((0,), (0,)), ((), ())), precision=lax.Precision.HIGHEST, preferred_element_type=jnp.float32)
    masses = lax.optimization_barrier(jnp.sum(weights, axis=0)) / balance
    new_centroids = moved * lax.rsqrt(lax.optimization_barrier(jnp.mean(moved * moved, axis=1, keepdims=True)) + 1e-06)
    return (new_centroids, masses)
```

```python
import jax
import jax.numpy as jnp
from jax import lax
from jax.sharding import Mesh
from jax.sharding import PartitionSpec as P

ITERS = 3


temper = 0.05

PTS_AXES = ("y", "c")
CEN_AXES = ("x", "z")


def unit_rows(values):
    wide = values.astype(jnp.float32)
    return (wide * lax.rsqrt(jnp.mean(wide * wide, axis=1, keepdims=True) + 1e-06)).astype(
        jnp.bfloat16
    )


def axis_sum(v, axis, n):
    if n == 1:
        return v
    got = [v] + [
        lax.ppermute(v, axis, [(i, (i + s) % n) for i in range(n)]) for s in range(1, n)
    ]
    if n == 2:
        return got[0] + got[1]
    if n == 4:
        return (got[0] + got[2]) + (got[1] + got[3])
    idx = lax.axis_index(axis)
    canon = jnp.stack(got)[(idx - jnp.arange(n)) % n]
    total = canon[0]
    for j in range(1, n):
        total = total + canon[j]
    return total


def multi_sum(v, axes):
    for axis, n in axes:
        v = axis_sum(v, axis, n)
    return v


def weighted_sum(weights, point_rows):
    return lax.dot_general(
        weights,
        point_rows.astype(jnp.float32),
        (((0,), (0,)), ((), ())),
        precision=lax.Precision.HIGHEST,
        preferred_element_type=jnp.float32,
    )


def make_local(sizes):
    pts_red = [("c", sizes["c"]), ("y", sizes["y"])]
    cen_red = [("z", sizes["z"]), ("x", sizes["x"])]

    def local(points, centroids):
        gathered = lax.all_gather(points, CEN_AXES, axis=1, tiled=True)
        unit_points = unit_rows(gathered)
        unit_centroids = unit_rows(centroids)
        width = gathered.shape[1]
        local_pts = gathered.shape[0]
        local_cen = centroids.shape[0]
        n_pts = sizes["y"] * sizes["c"]
        n_cen = sizes["x"] * sizes["z"]
        balance = local_pts * n_pts / (local_cen * n_cen)
        row_scale = jnp.ones((local_pts,), jnp.float32)
        col_scale = jnp.ones((local_cen,), jnp.float32)
        scores = jnp.dot(unit_points, unit_centroids.T, preferred_element_type=jnp.float32)
        kernel = jnp.exp(scores / (width * temper))
        for sweep in range(ITERS):
            col_part = jnp.sum(kernel * row_scale[:, None], axis=0)
            col_scale = balance / multi_sum(col_part, pts_red)
            row_part = jnp.sum(kernel * col_scale[None, :], axis=1)
            row_scale = 1.0 / multi_sum(row_part, cen_red)
        weights = row_scale[:, None] * kernel * col_scale[None, :]
        partial_value = weighted_sum(weights, gathered)
        mass_part = jnp.sum(weights, axis=0) / balance
        moved = lax.psum_scatter(partial_value, PTS_AXES, scatter_dimension=1, tiled=True)
        squares = jnp.sum(moved * moved, axis=1)
        both = multi_sum(jnp.stack([squares, mass_part]), pts_red)
        squares, masses = both[0], both[1]
        new_centroids = moved * lax.rsqrt(squares / width + 1e-06)[:, None]
        return (new_centroids, masses)

    return local


def solution(mesh):
    pts_n, cen_n = mesh.shape["pts"], mesh.shape["cen"]
    cores = 2 if pts_n % 2 == 0 else 1
    zs = 4 if cen_n % 4 == 0 else 1
    sizes = {"y": pts_n // cores, "c": cores, "x": cen_n // zs, "z": zs}
    mesh4 = Mesh(
        mesh.devices.reshape(sizes["y"], sizes["c"], sizes["x"], sizes["z"]),
        ("y", "c", "x", "z"),
    )
    in_specs = (P(PTS_AXES, CEN_AXES), P(CEN_AXES, None))
    out_specs = (P(CEN_AXES, PTS_AXES), P(CEN_AXES))
    return jax.shard_map(
        make_local(sizes), mesh=mesh4, in_specs=in_specs, out_specs=out_specs, check_vma=False
    )
```

```python
import jax
import jax.numpy as jnp
from jax import lax
from jax.sharding import Mesh
from jax.sharding import PartitionSpec as P

ITERS = 3
CHUNKS = 4


temper = 0.05

PTS_AXES = ("y", "c")
CEN_AXES = ("x", "z")


def unit_rows(values):
    wide = values.astype(jnp.float32)
    return (wide * lax.rsqrt(jnp.mean(wide * wide, axis=1, keepdims=True) + 1e-06)).astype(
        jnp.bfloat16
    )


def axis_sum(v, axis, n):
    if n == 1:
        return v
    got = [v] + [
        lax.ppermute(v, axis, [(i, (i + s) % n) for i in range(n)]) for s in range(1, n)
    ]
    if n == 2:
        return got[0] + got[1]
    if n == 4:
        return (got[0] + got[2]) + (got[1] + got[3])
    idx = lax.axis_index(axis)
    canon = jnp.stack(got)[(idx - jnp.arange(n)) % n]
    total = canon[0]
    for j in range(1, n):
        total = total + canon[j]
    return total


def multi_sum(v, axes):
    for axis, n in axes:
        v = axis_sum(v, axis, n)
    return v


def weighted_sum(weights, point_rows):
    return lax.dot_general(
        weights,
        point_rows.astype(jnp.float32),
        (((0,), (0,)), ((), ())),
        precision=lax.Precision.HIGHEST,
        preferred_element_type=jnp.float32,
    )


def make_local(sizes):
    pts_red = [("c", sizes["c"]), ("y", sizes["y"])]
    cen_red = [("z", sizes["z"]), ("x", sizes["x"])]

    def local(points, centroids):
        gathered = lax.all_gather(points, CEN_AXES, axis=1, tiled=True)
        unit_points = unit_rows(gathered)
        unit_centroids = unit_rows(centroids)
        width = gathered.shape[1]
        local_pts = gathered.shape[0]
        local_cen = centroids.shape[0]
        n_pts = sizes["y"] * sizes["c"]
        n_cen = sizes["x"] * sizes["z"]
        balance = local_pts * n_pts / (local_cen * n_cen)
        row_scale = jnp.ones((local_pts,), jnp.float32)
        col_scale = jnp.ones((local_cen,), jnp.float32)
        scores = jnp.dot(unit_points, unit_centroids.T, preferred_element_type=jnp.float32)
        kernel = jnp.exp(scores / (width * temper))
        for sweep in range(ITERS):
            col_part = jnp.sum(kernel * row_scale[:, None], axis=0)
            col_scale = balance / multi_sum(col_part, pts_red)
            row_part = jnp.sum(kernel * col_scale[None, :], axis=1)
            row_scale = 1.0 / multi_sum(row_part, cen_red)
        scaled = kernel * row_scale[:, None]
        hi = scaled.astype(jnp.bfloat16)
        lo = (scaled - hi.astype(jnp.float32)).astype(jnp.bfloat16)
        ones = jnp.ones((local_pts, 128), jnp.bfloat16)
        rhs = jnp.concatenate([gathered, ones], axis=1)
        chunks = CHUNKS if local_cen % (CHUNKS * 8) == 0 else 1
        step = local_cen // chunks
        moved_parts, mass_parts = [], []
        for j in range(chunks):
            cols = slice(j * step, (j + 1) * step)
            prod = lax.dot_general(
                hi[:, cols], rhs, (((0,), (0,)), ((), ())), preferred_element_type=jnp.float32
            ) + lax.dot_general(
                lo[:, cols], rhs, (((0,), (0,)), ((), ())), preferred_element_type=jnp.float32
            )
            prod = prod * col_scale[cols][:, None]
            mass_parts.append(prod[:, width])
            moved_parts.append(
                lax.psum_scatter(prod[:, :width], PTS_AXES, scatter_dimension=1, tiled=True)
            )
        moved = jnp.concatenate(moved_parts, axis=0)
        mass_part = jnp.concatenate(mass_parts) / balance
        squares = jnp.sum(moved * moved, axis=1)
        both = multi_sum(jnp.stack([squares, mass_part]), pts_red)
        squares, masses = both[0], both[1]
        new_centroids = moved * lax.rsqrt(squares / width + 1e-06)[:, None]
        return (new_centroids, masses)

    return local


def solution(mesh):
    pts_n, cen_n = mesh.shape["pts"], mesh.shape["cen"]
    cores = 2 if pts_n % 2 == 0 else 1
    zs = 4 if cen_n % 4 == 0 else 1
    sizes = {"y": pts_n // cores, "c": cores, "x": cen_n // zs, "z": zs}
    mesh4 = Mesh(
        mesh.devices.reshape(sizes["y"], sizes["c"], sizes["x"], sizes["z"]),
        ("y", "c", "x", "z"),
    )
    in_specs = (P(PTS_AXES, CEN_AXES), P(CEN_AXES, None))
    out_specs = (P(CEN_AXES, PTS_AXES), P(CEN_AXES))
    return jax.shard_map(
        make_local(sizes), mesh=mesh4, in_specs=in_specs, out_specs=out_specs, check_vma=False
    )
```

```python
import jax
import jax.numpy as jnp
from jax import lax
from jax.sharding import Mesh
from jax.sharding import PartitionSpec as P

ITERS = 3
CHUNKS = 2


temper = 0.05

PTS_AXES = ("y", "c")
CEN_AXES = ("x", "z")


def unit_rows(values):
    wide = values.astype(jnp.float32)
    return (wide * lax.rsqrt(jnp.mean(wide * wide, axis=1, keepdims=True) + 1e-06)).astype(
        jnp.bfloat16
    )


def axis_sum(v, axis, n):
    if n == 1:
        return v
    got = [v] + [
        lax.ppermute(v, axis, [(i, (i + s) % n) for i in range(n)]) for s in range(1, n)
    ]
    if n == 2:
        return got[0] + got[1]
    if n == 4:
        return (got[0] + got[2]) + (got[1] + got[3])
    idx = lax.axis_index(axis)
    canon = jnp.stack(got)[(idx - jnp.arange(n)) % n]
    total = canon[0]
    for j in range(1, n):
        total = total + canon[j]
    return total


def multi_sum(v, axes):
    for axis, n in axes:
        v = axis_sum(v, axis, n)
    return v


def weighted_sum(weights, point_rows):
    return lax.dot_general(
        weights,
        point_rows.astype(jnp.float32),
        (((0,), (0,)), ((), ())),
        precision=lax.Precision.HIGHEST,
        preferred_element_type=jnp.float32,
    )


def scatter_features(part_t, sizes):
    ny, nc = sizes["y"], sizes["c"]
    width, rows = part_t.shape
    blk = width // (ny * nc)
    x = part_t.reshape(ny, nc, blk, rows)
    if nc == 2:
        c = lax.axis_index("c")
        keep = lax.dynamic_index_in_dim(x, c, 1, keepdims=False)
        send = lax.dynamic_index_in_dim(x, 1 - c, 1, keepdims=False)
        x = keep + lax.ppermute(send, "c", [(0, 1), (1, 0)])
    else:
        x = x[:, 0]
    y = lax.axis_index("y")
    total = lax.dynamic_index_in_dim(x, y, 0, keepdims=False)
    for s in range(1, ny):
        piece = lax.dynamic_index_in_dim(x, (y + s) % ny, 0, keepdims=False)
        total = total + lax.ppermute(piece, "y", [(i, (i + s) % ny) for i in range(ny)])
    return total


def make_local(sizes):
    pts_red = [("c", sizes["c"]), ("y", sizes["y"])]
    cen_red = [("z", sizes["z"]), ("x", sizes["x"])]

    def local(points, centroids):
        gathered = lax.all_gather(points, CEN_AXES, axis=1, tiled=True)
        unit_points = unit_rows(gathered)
        unit_centroids = unit_rows(centroids)
        width = gathered.shape[1]
        local_pts = gathered.shape[0]
        local_cen = centroids.shape[0]
        n_pts = sizes["y"] * sizes["c"]
        n_cen = sizes["x"] * sizes["z"]
        balance = local_pts * n_pts / (local_cen * n_cen)
        row_scale = jnp.ones((local_pts,), jnp.float32)
        col_scale = jnp.ones((local_cen,), jnp.float32)
        scores = jnp.dot(unit_points, unit_centroids.T, preferred_element_type=jnp.float32)
        kernel = jnp.exp(scores / (width * temper))
        for sweep in range(ITERS):
            col_part = jnp.sum(kernel * row_scale[:, None], axis=0)
            col_scale = balance / multi_sum(col_part, pts_red)
            row_part = jnp.sum(kernel * col_scale[None, :], axis=1)
            row_scale = 1.0 / multi_sum(row_part, cen_red)
        weights = row_scale[:, None] * kernel * col_scale[None, :]
        ones = jnp.ones((local_pts, 8), jnp.float32)
        lhs = jnp.concatenate([gathered.astype(jnp.float32), ones], axis=1)
        chunks = CHUNKS if local_cen % (CHUNKS * 128) == 0 else 1
        step = local_cen // chunks
        moved_parts, mass_parts = [], []
        for j in range(chunks):
            cols = slice(j * step, (j + 1) * step)
            prod = lax.dot_general(
                lhs,
                weights[:, cols],
                (((0,), (0,)), ((), ())),
                precision=lax.Precision.HIGHEST,
                preferred_element_type=jnp.float32,
            )
            mass_parts.append(prod[width])
            moved_parts.append(scatter_features(prod[:width], sizes).T)
        moved = jnp.concatenate(moved_parts, axis=0)
        mass_part = jnp.concatenate(mass_parts) / balance
        squares = jnp.sum(moved * moved, axis=1)
        both = multi_sum(jnp.stack([squares, mass_part]), pts_red)
        squares, masses = both[0], both[1]
        new_centroids = moved * lax.rsqrt(squares / width + 1e-06)[:, None]
        return (new_centroids, masses)

    return local


def solution(mesh):
    pts_n, cen_n = mesh.shape["pts"], mesh.shape["cen"]
    cores = 2 if pts_n % 2 == 0 else 1
    zs = 4 if cen_n % 4 == 0 else 1
    sizes = {"y": pts_n // cores, "c": cores, "x": cen_n // zs, "z": zs}
    mesh4 = Mesh(
        mesh.devices.reshape(sizes["y"], sizes["c"], sizes["x"], sizes["z"]),
        ("y", "c", "x", "z"),
    )
    in_specs = (P(PTS_AXES, CEN_AXES), P(CEN_AXES, None))
    out_specs = (P(CEN_AXES, PTS_AXES), P(CEN_AXES))
    return jax.shard_map(
        make_local(sizes), mesh=mesh4, in_specs=in_specs, out_specs=out_specs, check_vma=False
    )
```

```python
import jax
import jax.numpy as jnp
from jax import lax
from jax.sharding import Mesh
from jax.sharding import PartitionSpec as P

ITERS = 3


temper = 0.05

PTS_AXES = ("y", "c")
CEN_AXES = ("x", "z")


def unit_rows(values):
    wide = values.astype(jnp.float32)
    return (wide * lax.rsqrt(jnp.mean(wide * wide, axis=1, keepdims=True) + 1e-06)).astype(
        jnp.bfloat16
    )


def axis_sum(v, axis, n):
    if n == 1:
        return v
    got = [v] + [
        lax.ppermute(v, axis, [(i, (i + s) % n) for i in range(n)]) for s in range(1, n)
    ]
    if n == 2:
        return got[0] + got[1]
    if n == 4:
        return (got[0] + got[2]) + (got[1] + got[3])
    idx = lax.axis_index(axis)
    canon = jnp.stack(got)[(idx - jnp.arange(n)) % n]
    total = canon[0]
    for j in range(1, n):
        total = total + canon[j]
    return total


def multi_sum(v, axes):
    for axis, n in axes:
        v = axis_sum(v, axis, n)
    return v


def weighted_sum(weights, point_rows):
    return lax.dot_general(
        weights,
        point_rows.astype(jnp.float32),
        (((0,), (0,)), ((), ())),
        precision=lax.Precision.HIGHEST,
        preferred_element_type=jnp.float32,
    )


def scatter_features(part_t, sizes):
    ny, nc = sizes["y"], sizes["c"]
    width, rows = part_t.shape
    blk = width // (ny * nc)
    x = part_t.reshape(ny, nc, blk, rows)
    if nc == 2:
        c = lax.axis_index("c")
        keep = lax.dynamic_index_in_dim(x, c, 1, keepdims=False)
        send = lax.dynamic_index_in_dim(x, 1 - c, 1, keepdims=False)
        x = keep + lax.ppermute(send, "c", [(0, 1), (1, 0)])
    else:
        x = x[:, 0]
    if ny == 1:
        return x[0]
    got = lax.all_to_all(x, "y", 0, 0, tiled=False)
    total = got[0]
    for j in range(1, ny):
        total = total + got[j]
    return total


def gather_features(points, sizes):
    n = sizes["x"] * sizes["z"]
    rows, blk = points.shape
    if n == 1:
        return points
    sent = jnp.broadcast_to(points[None], (n, rows, blk))
    got = lax.all_to_all(sent, CEN_AXES, 0, 0, tiled=False)
    return jnp.transpose(got, (1, 0, 2)).reshape(rows, n * blk)


def make_local(sizes):
    pts_red = [("c", sizes["c"]), ("y", sizes["y"])]
    cen_red = [("z", sizes["z"]), ("x", sizes["x"])]

    def local(points, centroids):
        gathered = gather_features(points, sizes)
        unit_points = unit_rows(gathered)
        unit_centroids = unit_rows(centroids)
        width = gathered.shape[1]
        local_pts = gathered.shape[0]
        local_cen = centroids.shape[0]
        n_pts = sizes["y"] * sizes["c"]
        n_cen = sizes["x"] * sizes["z"]
        balance = local_pts * n_pts / (local_cen * n_cen)
        row_scale = jnp.ones((local_pts,), jnp.float32)
        col_scale = jnp.ones((local_cen,), jnp.float32)
        scores = jnp.dot(unit_points, unit_centroids.T, preferred_element_type=jnp.float32)
        kernel = jnp.exp(scores / (width * temper))
        for sweep in range(ITERS):
            col_part = jnp.sum(kernel * row_scale[:, None], axis=0)
            col_scale = balance / multi_sum(col_part, pts_red)
            row_part = jnp.sum(kernel * col_scale[None, :], axis=1)
            row_scale = 1.0 / multi_sum(row_part, cen_red)
        weights = row_scale[:, None] * kernel * col_scale[None, :]
        partial_value = weighted_sum(weights, gathered)
        mass_part = jnp.sum(weights, axis=0) / balance
        moved = scatter_features(partial_value.T, sizes).T
        squares = jnp.sum(moved * moved, axis=1)
        both = multi_sum(jnp.stack([squares, mass_part]), pts_red)
        squares, masses = both[0], both[1]
        new_centroids = moved * lax.rsqrt(squares / width + 1e-06)[:, None]
        return (new_centroids, masses)

    return local


def solution(mesh):
    pts_n, cen_n = mesh.shape["pts"], mesh.shape["cen"]
    cores = 2 if pts_n % 2 == 0 else 1
    zs = 4 if cen_n % 4 == 0 else 1
    sizes = {"y": pts_n // cores, "c": cores, "x": cen_n // zs, "z": zs}
    mesh4 = Mesh(
        mesh.devices.reshape(sizes["y"], sizes["c"], sizes["x"], sizes["z"]),
        ("y", "c", "x", "z"),
    )
    in_specs = (P(PTS_AXES, CEN_AXES), P(CEN_AXES, None))
    out_specs = (P(CEN_AXES, PTS_AXES), P(CEN_AXES))
    return jax.shard_map(
        make_local(sizes), mesh=mesh4, in_specs=in_specs, out_specs=out_specs, check_vma=False
    )
```

```python
import jax
import jax.numpy as jnp
from jax import lax
from jax.sharding import Mesh

from jax.sharding import PartitionSpec as P

ITERS = 3
CHUNKS = 2


temper = 0.05

PTS_AXES = ("y", "c")
CEN_AXES = ("x", "z")


def unit_rows(values):
    wide = values.astype(jnp.float32)
    return (wide * lax.rsqrt(jnp.mean(wide * wide, axis=1, keepdims=True) + 1e-06)).astype(
        jnp.bfloat16
    )


def axis_sum(v, axis, n):
    if n == 1:
        return v
    got = [v] + [
        lax.ppermute(v, axis, [(i, (i + s) % n) for i in range(n)]) for s in range(1, n)
    ]
    if n == 2:
        return got[0] + got[1]
    if n == 4:
        return (got[0] + got[2]) + (got[1] + got[3])
    idx = lax.axis_index(axis)
    canon = jnp.stack(got)[(idx - jnp.arange(n)) % n]
    total = canon[0]
    for j in range(1, n):
        total = total + canon[j]
    return total


def multi_sum(v, axes):
    for axis, n in axes:
        v = axis_sum(v, axis, n)
    return v


def weighted_sum(weights, point_rows):
    return lax.dot_general(
        weights,
        point_rows.astype(jnp.float32),
        (((0,), (0,)), ((), ())),
        precision=lax.Precision.HIGHEST,
        preferred_element_type=jnp.float32,
    )


def scatter_features(part_t, sizes):
    ny, nc = sizes["y"], sizes["c"]
    width, rows = part_t.shape
    blk = width // (ny * nc)
    x = part_t.reshape(ny, nc, blk, rows)
    if nc == 2:
        c = lax.axis_index("c")
        keep = lax.dynamic_index_in_dim(x, c, 1, keepdims=False)
        send = lax.dynamic_index_in_dim(x, 1 - c, 1, keepdims=False)
        x = keep + lax.ppermute(send, "c", [(0, 1), (1, 0)])
    else:
        x = x[:, 0]
    if ny == 1:
        return x[0]
    got = lax.all_to_all(x, "y", 0, 0, tiled=False)
    total = got[0]
    for j in range(1, ny):
        total = total + got[j]
    return total


def gather_features(points, sizes):
    n = sizes["x"] * sizes["z"]
    rows, blk = points.shape
    if n == 1:
        return points
    sent = jnp.broadcast_to(points[None], (n, rows, blk))
    got = lax.all_to_all(sent, CEN_AXES, 0, 0, tiled=False)
    return jnp.transpose(got, (1, 0, 2)).reshape(rows, n * blk)


def make_local(sizes):
    pts_red = [("c", sizes["c"]), ("y", sizes["y"])]
    cen_red = [("z", sizes["z"]), ("x", sizes["x"])]

    def local(points, centroids):
        gathered = gather_features(points, sizes)
        unit_points = unit_rows(gathered)
        unit_centroids = unit_rows(centroids)
        width = gathered.shape[1]
        local_pts = gathered.shape[0]
        local_cen = centroids.shape[0]
        n_pts = sizes["y"] * sizes["c"]
        n_cen = sizes["x"] * sizes["z"]
        balance = local_pts * n_pts / (local_cen * n_cen)
        row_scale = jnp.ones((local_pts,), jnp.float32)
        col_scale = jnp.ones((local_cen,), jnp.float32)
        scores = jnp.dot(unit_points, unit_centroids.T, preferred_element_type=jnp.float32)
        kernel = jnp.exp(scores / (width * temper))
        for _ in range(ITERS):
            col_part = jnp.sum(kernel * row_scale[:, None], axis=0)
            col_scale = balance / multi_sum(col_part, pts_red)
            row_part = jnp.sum(kernel * col_scale[None, :], axis=1)
            row_scale = 1.0 / multi_sum(row_part, cen_red)
        weights = row_scale[:, None] * kernel * col_scale[None, :]
        mass_part = jnp.sum(weights, axis=0) / balance
        chunks = CHUNKS if local_cen % (CHUNKS * 128) == 0 else 1
        step = local_cen // chunks
        moved_parts = []
        for j in range(chunks):
            partial_value = weighted_sum(weights[:, j * step:(j + 1) * step], gathered)
            moved_parts.append(scatter_features(partial_value.T, sizes).T)
        moved = jnp.concatenate(moved_parts, axis=0)
        squares = jnp.sum(moved * moved, axis=1)
        both = multi_sum(jnp.stack([squares, mass_part]), pts_red)
        squares, masses = both[0], both[1]
        new_centroids = moved * lax.rsqrt(squares / width + 1e-06)[:, None]
        return (new_centroids, masses)

    return local


def solution(mesh):
    pts_n, cen_n = mesh.shape["pts"], mesh.shape["cen"]
    cores = 2 if pts_n % 2 == 0 else 1
    zs = 4 if cen_n % 4 == 0 else 1
    sizes = {"y": pts_n // cores, "c": cores, "x": cen_n // zs, "z": zs}
    mesh4 = Mesh(
        mesh.devices.reshape(sizes["y"], sizes["c"], sizes["x"], sizes["z"]),
        ("y", "c", "x", "z"),
    )
    in_specs = (P(PTS_AXES, CEN_AXES), P(CEN_AXES, None))
    out_specs = (P(CEN_AXES, PTS_AXES), P(CEN_AXES))
    return jax.shard_map(
        make_local(sizes), mesh=mesh4, in_specs=in_specs, out_specs=out_specs, check_vma=False
    )
```

```python
import jax
import jax.numpy as jnp
from jax import lax
from jax.sharding import Mesh
from jax.sharding import PartitionSpec as P

ITERS = 3


temper = 0.05

PTS_AXES = ("y", "c")
CEN_AXES = ("x", "z")


def unit_rows(values):
    wide = values.astype(jnp.float32)
    return (wide * lax.rsqrt(jnp.mean(wide * wide, axis=1, keepdims=True) + 1e-06)).astype(
        jnp.bfloat16
    )


def axis_sum(v, axis, n):
    if n == 1:
        return v
    got = [v] + [
        lax.ppermute(v, axis, [(i, (i + s) % n) for i in range(n)]) for s in range(1, n)
    ]
    if n == 2:
        return got[0] + got[1]
    if n == 4:
        return (got[0] + got[2]) + (got[1] + got[3])
    idx = lax.axis_index(axis)
    canon = jnp.stack(got)[(idx - jnp.arange(n)) % n]
    total = canon[0]
    for j in range(1, n):
        total = total + canon[j]
    return total


def multi_sum(v, axes):
    for axis, n in axes:
        v = axis_sum(v, axis, n)
    return v


def weighted_sum(weights, point_rows):
    return lax.dot_general(
        weights,
        point_rows.astype(jnp.float32),
        (((0,), (0,)), ((), ())),
        precision=lax.Precision.HIGHEST,
        preferred_element_type=jnp.float32,
    )


def scatter_features(part_t, sizes):
    ny, nc = sizes["y"], sizes["c"]
    width, rows = part_t.shape
    blk = width // (ny * nc)
    x = part_t.reshape(ny, nc, blk, rows)
    if nc == 2:
        c = lax.axis_index("c")
        keep = lax.dynamic_index_in_dim(x, c, 1, keepdims=False)
        send = lax.dynamic_index_in_dim(x, 1 - c, 1, keepdims=False)
        x = keep + lax.ppermute(send, "c", [(0, 1), (1, 0)])
    else:
        x = x[:, 0]
    if ny == 1:
        return x[0]
    got = lax.all_to_all(x, "y", 0, 0, tiled=False)
    total = got[0]
    for j in range(1, ny):
        total = total + got[j]
    return total


def gather_features(points, sizes):
    n = sizes["x"] * sizes["z"]
    rows, blk = points.shape
    if n == 1:
        return points
    sent = jnp.broadcast_to(points[None], (n, rows, blk))
    got = lax.all_to_all(sent, CEN_AXES, 0, 0, tiled=False)
    return jnp.transpose(got, (1, 0, 2)).reshape(rows, n * blk)


def make_local(sizes):
    pts_red = [("c", sizes["c"]), ("y", sizes["y"])]
    cen_red = [("z", sizes["z"]), ("x", sizes["x"])]

    def local(points, centroids):
        gathered = gather_features(points, sizes)
        unit_points = unit_rows(gathered)
        unit_centroids = unit_rows(centroids)
        width = gathered.shape[1]
        local_pts = gathered.shape[0]
        local_cen = centroids.shape[0]
        n_pts = sizes["y"] * sizes["c"]
        n_cen = sizes["x"] * sizes["z"]
        balance = local_pts * n_pts / (local_cen * n_cen)
        row_scale = jnp.ones((local_pts,), jnp.float32)
        col_scale = jnp.ones((local_cen,), jnp.float32)
        scores = jnp.dot(unit_points, unit_centroids.T, preferred_element_type=jnp.float32)
        kernel = jnp.exp(scores / (width * temper))
        for sweep in range(ITERS):
            col_part = jnp.sum(kernel * row_scale[:, None], axis=0)
            col_scale = balance / multi_sum(col_part, pts_red)
            row_part = jnp.sum(kernel * col_scale[None, :], axis=1)
            row_scale = 1.0 / multi_sum(row_part, cen_red)
        scaled = kernel * row_scale[:, None]
        hi_wide = lax.reduce_precision(scaled, exponent_bits=8, mantissa_bits=7)
        hi = hi_wide.astype(jnp.bfloat16)
        lo = (scaled - hi_wide).astype(jnp.bfloat16)
        dims = (((0,), (0,)), ((), ()))
        partial_t = lax.dot_general(
            gathered, hi, dims, preferred_element_type=jnp.float32
        ) + lax.dot_general(gathered, lo, dims, preferred_element_type=jnp.float32)
        partial_t = partial_t * col_scale[None, :]
        mass_part = jnp.sum(scaled, axis=0) * col_scale / balance
        moved = scatter_features(partial_t, sizes).T
        squares = jnp.sum(moved * moved, axis=1)
        both = multi_sum(jnp.stack([squares, mass_part]), pts_red)
        squares, masses = both[0], both[1]
        new_centroids = moved * lax.rsqrt(squares / width + 1e-06)[:, None]
        return (new_centroids, masses)

    return local


def solution(mesh):
    pts_n, cen_n = mesh.shape["pts"], mesh.shape["cen"]
    cores = 2 if pts_n % 2 == 0 else 1
    zs = 4 if cen_n % 4 == 0 else 1
    sizes = {"y": pts_n // cores, "c": cores, "x": cen_n // zs, "z": zs}
    mesh4 = Mesh(
        mesh.devices.reshape(sizes["y"], sizes["c"], sizes["x"], sizes["z"]),
        ("y", "c", "x", "z"),
    )
    in_specs = (P(PTS_AXES, CEN_AXES), P(CEN_AXES, None))
    out_specs = (P(CEN_AXES, PTS_AXES), P(CEN_AXES))
    return jax.shard_map(
        make_local(sizes), mesh=mesh4, in_specs=in_specs, out_specs=out_specs, check_vma=False
    )
```

```python
import jax
import jax.numpy as jnp
from jax import lax
from jax.sharding import Mesh
from jax.sharding import PartitionSpec as P

ITERS = 3


temper = 0.05

PTS_AXES = ("y", "c")
CEN_AXES = ("x", "z")


def unit_rows(values):
    wide = values.astype(jnp.float32)
    return (wide * lax.rsqrt(jnp.mean(wide * wide, axis=1, keepdims=True) + 1e-06)).astype(
        jnp.bfloat16
    )


def axis_sum(v, axis, n):
    if n == 1:
        return v
    got = [v] + [
        lax.ppermute(v, axis, [(i, (i + s) % n) for i in range(n)]) for s in range(1, n)
    ]
    if n == 2:
        return got[0] + got[1]
    if n == 4:
        return (got[0] + got[2]) + (got[1] + got[3])
    idx = lax.axis_index(axis)
    canon = jnp.stack(got)[(idx - jnp.arange(n)) % n]
    total = canon[0]
    for j in range(1, n):
        total = total + canon[j]
    return total


def group_sum(v, axes, n):
    if n == 1:
        return v
    got = lax.all_to_all(jnp.broadcast_to(v[None], (n,) + v.shape), axes, 0, 0, tiled=False)
    total = got[0]
    for j in range(1, n):
        total = total + got[j]
    return total


def multi_sum(v, axes):
    for axis, n in axes:
        v = axis_sum(v, axis, n)
    return v


def weighted_sum(weights, point_rows):
    return lax.dot_general(
        weights,
        point_rows.astype(jnp.float32),
        (((0,), (0,)), ((), ())),
        precision=lax.Precision.HIGHEST,
        preferred_element_type=jnp.float32,
    )


def scatter_features(part_t, sizes):
    ny, nc = sizes["y"], sizes["c"]
    width, rows = part_t.shape
    blk = width // (ny * nc)
    x = part_t.reshape(ny, nc, blk, rows)
    if nc == 2:
        c = lax.axis_index("c")
        keep = lax.dynamic_index_in_dim(x, c, 1, keepdims=False)
        send = lax.dynamic_index_in_dim(x, 1 - c, 1, keepdims=False)
        x = keep + lax.ppermute(send, "c", [(0, 1), (1, 0)])
    else:
        x = x[:, 0]
    if ny == 1:
        return x[0]
    got = lax.all_to_all(x, "y", 0, 0, tiled=False)
    total = got[0]
    for j in range(1, ny):
        total = total + got[j]
    return total


def gather_features(points, sizes):
    n = sizes["x"] * sizes["z"]
    rows, blk = points.shape
    if n == 1:
        return points
    sent = jnp.broadcast_to(points[None], (n, rows, blk))
    got = lax.all_to_all(sent, CEN_AXES, 0, 0, tiled=False)
    return jnp.transpose(got, (1, 0, 2)).reshape(rows, n * blk)


def make_local(sizes):
    pts_red = [("c", sizes["c"]), ("y", sizes["y"])]
    cen_red = [("z", sizes["z"]), ("x", sizes["x"])]

    def local(points, centroids):
        gathered = gather_features(points, sizes)
        unit_points = unit_rows(gathered)
        unit_centroids = unit_rows(centroids)
        width = gathered.shape[1]
        local_pts = gathered.shape[0]
        local_cen = centroids.shape[0]
        n_pts = sizes["y"] * sizes["c"]
        n_cen = sizes["x"] * sizes["z"]
        balance = local_pts * n_pts / (local_cen * n_cen)
        row_scale = jnp.ones((local_pts,), jnp.float32)
        col_scale = jnp.ones((local_cen,), jnp.float32)
        scores = jnp.dot(unit_points, unit_centroids.T, preferred_element_type=jnp.float32)
        kernel = jnp.exp(scores / (width * temper))
        for sweep in range(ITERS):
            col_part = jnp.sum(kernel * row_scale[:, None], axis=0)
            col_scale = balance / multi_sum(col_part, pts_red)
            row_part = jnp.sum(kernel * col_scale[None, :], axis=1)
            row_scale = 1.0 / group_sum(row_part, CEN_AXES, n_cen)
        scaled = kernel * row_scale[:, None]
        hi_wide = lax.reduce_precision(scaled, exponent_bits=8, mantissa_bits=7)
        hi = hi_wide.astype(jnp.bfloat16)
        lo = (scaled - hi_wide).astype(jnp.bfloat16)
        dims = (((0,), (0,)), ((), ()))
        partial_t = lax.dot_general(
            gathered, hi, dims, preferred_element_type=jnp.float32
        ) + lax.dot_general(gathered, lo, dims, preferred_element_type=jnp.float32)
        partial_t = partial_t * col_scale[None, :]
        mass_part = jnp.sum(scaled, axis=0) * col_scale / balance
        moved = scatter_features(partial_t, sizes).T
        squares = jnp.sum(moved * moved, axis=1)
        both = multi_sum(jnp.stack([squares, mass_part]), pts_red)
        squares, masses = both[0], both[1]
        new_centroids = moved * lax.rsqrt(squares / width + 1e-06)[:, None]
        return (new_centroids, masses)

    return local


def solution(mesh):
    pts_n, cen_n = mesh.shape["pts"], mesh.shape["cen"]
    cores = 2 if pts_n % 2 == 0 else 1
    zs = 4 if cen_n % 4 == 0 else 1
    sizes = {"y": pts_n // cores, "c": cores, "x": cen_n // zs, "z": zs}
    mesh4 = Mesh(
        mesh.devices.reshape(sizes["y"], sizes["c"], sizes["x"], sizes["z"]),
        ("y", "c", "x", "z"),
    )
    in_specs = (P(PTS_AXES, CEN_AXES), P(CEN_AXES, None))
    out_specs = (P(CEN_AXES, PTS_AXES), P(CEN_AXES))
    return jax.shard_map(
        make_local(sizes), mesh=mesh4, in_specs=in_specs, out_specs=out_specs, check_vma=False
    )
```

```python
import jax
import jax.numpy as jnp
from jax import lax
from jax.sharding import Mesh
from jax.sharding import PartitionSpec as P

ITERS = 3


temper = 0.05

PTS_AXES = ("y", "c")
CEN_AXES = ("x", "z")


def unit_rows(values):
    wide = values.astype(jnp.float32)
    return (wide * lax.rsqrt(jnp.mean(wide * wide, axis=1, keepdims=True) + 1e-06)).astype(
        jnp.bfloat16
    )


def axis_sum(v, axis, n):
    if n == 1:
        return v
    got = [v] + [
        lax.ppermute(v, axis, [(i, (i + s) % n) for i in range(n)]) for s in range(1, n)
    ]
    if n == 2:
        return got[0] + got[1]
    if n == 4:
        return (got[0] + got[2]) + (got[1] + got[3])
    idx = lax.axis_index(axis)
    canon = jnp.stack(got)[(idx - jnp.arange(n)) % n]
    total = canon[0]
    for j in range(1, n):
        total = total + canon[j]
    return total


def group_sum(v, axes, n):
    if n == 1:
        return v
    got = lax.all_to_all(jnp.broadcast_to(v[None], (n,) + v.shape), axes, 0, 0, tiled=False)
    total = got[0]
    for j in range(1, n):
        total = total + got[j]
    return total


def multi_sum(v, axes):
    for axis, n in axes:
        v = axis_sum(v, axis, n)
    return v


def weighted_sum(weights, point_rows):
    return lax.dot_general(
        weights,
        point_rows.astype(jnp.float32),
        (((0,), (0,)), ((), ())),
        precision=lax.Precision.HIGHEST,
        preferred_element_type=jnp.float32,
    )


def scatter_features(part_t, sizes):
    ny, nc = sizes["y"], sizes["c"]
    width, rows = part_t.shape
    blk = width // (ny * nc)
    x = part_t.reshape(ny, nc, blk, rows)
    if nc == 2:
        c = lax.axis_index("c")
        keep = lax.dynamic_index_in_dim(x, c, 1, keepdims=False)
        send = lax.dynamic_index_in_dim(x, 1 - c, 1, keepdims=False)
        x = keep + lax.ppermute(send, "c", [(0, 1), (1, 0)])
    else:
        x = x[:, 0]
    if ny == 1:
        return x[0]
    got = lax.all_to_all(x, "y", 0, 0, tiled=False)
    total = got[0]
    for j in range(1, ny):
        total = total + got[j]
    return total


def ring_gather(v, axis, n):
    if n == 1:
        return v[None]
    if n != 4:
        return lax.all_to_all(jnp.broadcast_to(v[None], (n,) + v.shape), axis, 0, 0, tiled=False)
    fwd = lax.ppermute(v, axis, [(i, (i + 1) % n) for i in range(n)])
    bwd = lax.ppermute(v, axis, [(i, (i - 1) % n) for i in range(n)])
    half = v.shape[-2] // 2
    far = jnp.concatenate(
        [
            lax.ppermute(fwd[..., :half, :], axis, [(i, (i + 1) % n) for i in range(n)]),
            lax.ppermute(bwd[..., half:, :], axis, [(i, (i - 1) % n) for i in range(n)]),
        ],
        axis=-2,
    )
    by_offset = jnp.stack([v, fwd, far, bwd])
    idx = lax.axis_index(axis)
    return by_offset[(idx - jnp.arange(n)) % n]


def gather_features(points, sizes):
    nx, nz = sizes["x"], sizes["z"]
    rows, blk = points.shape
    if nx * nz == 1:
        return points
    if blk % 2 or rows % 2:
        got = lax.all_to_all(
            jnp.broadcast_to(points[None], (nx * nz, rows, blk)), CEN_AXES, 0, 0, tiled=False
        )
        return jnp.transpose(got, (1, 0, 2)).reshape(rows, nx * nz * blk)
    part_a, part_b = points[:, : blk // 2], points[:, blk // 2 :]
    a_z = ring_gather(part_a, "z", nz)
    b_x = ring_gather(part_b, "x", nx)
    a_xz = ring_gather(a_z, "x", nx)
    b_zx = ring_gather(b_x, "z", nz)
    full = jnp.concatenate([a_xz, jnp.transpose(b_zx, (1, 0, 2, 3))], axis=-1)
    return jnp.transpose(full, (2, 0, 1, 3)).reshape(rows, nx * nz * blk)


def make_local(sizes):
    pts_red = [("c", sizes["c"]), ("y", sizes["y"])]
    cen_red = [("z", sizes["z"]), ("x", sizes["x"])]

    def local(points, centroids):
        gathered = gather_features(points, sizes)
        unit_points = unit_rows(gathered)
        unit_centroids = unit_rows(centroids)
        width = gathered.shape[1]
        local_pts = gathered.shape[0]
        local_cen = centroids.shape[0]
        n_pts = sizes["y"] * sizes["c"]
        n_cen = sizes["x"] * sizes["z"]
        balance = local_pts * n_pts / (local_cen * n_cen)
        row_scale = jnp.ones((local_pts,), jnp.float32)
        col_scale = jnp.ones((local_cen,), jnp.float32)
        scores = jnp.dot(unit_points, unit_centroids.T, preferred_element_type=jnp.float32)
        kernel = jnp.exp(scores / (width * temper))
        for sweep in range(ITERS):
            col_part = jnp.sum(kernel * row_scale[:, None], axis=0)
            col_scale = balance / multi_sum(col_part, pts_red)
            row_part = jnp.sum(kernel * col_scale[None, :], axis=1)
            row_scale = 1.0 / group_sum(row_part, CEN_AXES, n_cen)
        scaled = kernel * row_scale[:, None]
        hi_wide = lax.reduce_precision(scaled, exponent_bits=8, mantissa_bits=7)
        hi = hi_wide.astype(jnp.bfloat16)
        lo = (scaled - hi_wide).astype(jnp.bfloat16)
        dims = (((0,), (0,)), ((), ()))
        partial_t = lax.dot_general(
            gathered, hi, dims, preferred_element_type=jnp.float32
        ) + lax.dot_general(gathered, lo, dims, preferred_element_type=jnp.float32)
        partial_t = partial_t * col_scale[None, :]
        mass_part = jnp.sum(scaled, axis=0) * col_scale / balance
        moved = scatter_features(partial_t, sizes).T
        squares = jnp.sum(moved * moved, axis=1)
        both = multi_sum(jnp.stack([squares, mass_part]), pts_red)
        squares, masses = both[0], both[1]
        new_centroids = moved * lax.rsqrt(squares / width + 1e-06)[:, None]
        return (new_centroids, masses)

    return local


def solution(mesh):
    pts_n, cen_n = mesh.shape["pts"], mesh.shape["cen"]
    cores = 2 if pts_n % 2 == 0 else 1
    zs = 4 if cen_n % 4 == 0 else 1
    sizes = {"y": pts_n // cores, "c": cores, "x": cen_n // zs, "z": zs}
    mesh4 = Mesh(
        mesh.devices.reshape(sizes["y"], sizes["c"], sizes["x"], sizes["z"]),
        ("y", "c", "x", "z"),
    )
    in_specs = (P(PTS_AXES, CEN_AXES), P(CEN_AXES, None))
    out_specs = (P(CEN_AXES, PTS_AXES), P(CEN_AXES))
    return jax.shard_map(
        make_local(sizes), mesh=mesh4, in_specs=in_specs, out_specs=out_specs, check_vma=False
    )
```

```python
import jax
import jax.numpy as jnp
from jax import lax
from jax.sharding import Mesh
from jax.sharding import PartitionSpec as P

ITERS = 3


temper = 0.05

PTS_AXES = ("y", "c")
CEN_AXES = ("x", "z")


def unit_rows(values):
    wide = values.astype(jnp.float32)
    return (wide * lax.rsqrt(jnp.mean(wide * wide, axis=1, keepdims=True) + 1e-06)).astype(
        jnp.bfloat16
    )


def axis_sum(v, axis, n):
    if n == 1:
        return v
    got = [v] + [
        lax.ppermute(v, axis, [(i, (i + s) % n) for i in range(n)]) for s in range(1, n)
    ]
    if n == 2:
        return got[0] + got[1]
    if n == 4:
        return (got[0] + got[2]) + (got[1] + got[3])
    idx = lax.axis_index(axis)
    canon = jnp.stack(got)[(idx - jnp.arange(n)) % n]
    total = canon[0]
    for j in range(1, n):
        total = total + canon[j]
    return total


def group_sum(v, axes, n):
    if n == 1:
        return v
    got = lax.all_to_all(jnp.broadcast_to(v[None], (n,) + v.shape), axes, 0, 0, tiled=False)
    total = got[0]
    for j in range(1, n):
        total = total + got[j]
    return total


def multi_sum(v, axes):
    for axis, n in axes:
        v = axis_sum(v, axis, n)
    return v


def weighted_sum(weights, point_rows):
    return lax.dot_general(
        weights,
        point_rows.astype(jnp.float32),
        (((0,), (0,)), ((), ())),
        precision=lax.Precision.HIGHEST,
        preferred_element_type=jnp.float32,
    )


def scatter_product(point_rows, hi, lo, col_scale, sizes):
    ny, nc = sizes["y"], sizes["c"]
    rows, width = point_rows.shape
    blk = width // (ny * nc)
    dims = (((0,), (0,)), ((), ()))

    def product(cols):
        part = lax.dot_general(cols, hi, dims, preferred_element_type=jnp.float32)
        part = part + lax.dot_general(cols, lo, dims, preferred_element_type=jnp.float32)
        return part * col_scale[None, :]

    split = point_rows.reshape(rows, ny, nc, blk)
    if nc == 2:
        c = lax.axis_index("c")
        send = lax.dynamic_index_in_dim(split, 1 - c, 2, keepdims=False)
        keep = lax.dynamic_index_in_dim(split, c, 2, keepdims=False)
        sent = product(send.reshape(rows, ny * blk))
        got = lax.ppermute(sent, "c", [(0, 1), (1, 0)])
        x = product(keep.reshape(rows, ny * blk)) + got
    else:
        x = product(split[:, :, 0].reshape(rows, ny * blk))
    x = x.reshape(ny, blk, -1)
    if ny == 1:
        return x[0]
    got = lax.all_to_all(x, "y", 0, 0, tiled=False)
    total = got[0]
    for j in range(1, ny):
        total = total + got[j]
    return total


def ring_gather(v, axis, n):
    if n == 1:
        return v[None]
    if n != 4:
        return lax.all_to_all(jnp.broadcast_to(v[None], (n,) + v.shape), axis, 0, 0, tiled=False)
    fwd = lax.ppermute(v, axis, [(i, (i + 1) % n) for i in range(n)])
    bwd = lax.ppermute(v, axis, [(i, (i - 1) % n) for i in range(n)])
    half = v.shape[-2] // 2
    far = jnp.concatenate(
        [
            lax.ppermute(fwd[..., :half, :], axis, [(i, (i + 1) % n) for i in range(n)]),
            lax.ppermute(bwd[..., half:, :], axis, [(i, (i - 1) % n) for i in range(n)]),
        ],
        axis=-2,
    )
    by_offset = jnp.stack([v, fwd, far, bwd])
    idx = lax.axis_index(axis)
    return by_offset[(idx - jnp.arange(n)) % n]


def gather_features(points, sizes):
    nx, nz = sizes["x"], sizes["z"]
    rows, blk = points.shape
    if nx * nz == 1:
        return points
    if blk % 2 or rows % 2:
        got = lax.all_to_all(
            jnp.broadcast_to(points[None], (nx * nz, rows, blk)), CEN_AXES, 0, 0, tiled=False
        )
        return jnp.transpose(got, (1, 0, 2)).reshape(rows, nx * nz * blk)
    part_a, part_b = points[:, : blk // 2], points[:, blk // 2 :]
    a_z = ring_gather(part_a, "z", nz)
    b_x = ring_gather(part_b, "x", nx)
    a_xz = ring_gather(a_z, "x", nx)
    b_zx = ring_gather(b_x, "z", nz)
    full = jnp.concatenate([a_xz, jnp.transpose(b_zx, (1, 0, 2, 3))], axis=-1)
    return jnp.transpose(full, (2, 0, 1, 3)).reshape(rows, nx * nz * blk)


def make_local(sizes):
    pts_red = [("c", sizes["c"]), ("y", sizes["y"])]
    cen_red = [("z", sizes["z"]), ("x", sizes["x"])]

    def local(points, centroids):
        gathered = gather_features(points, sizes)
        unit_points = unit_rows(gathered)
        unit_centroids = unit_rows(centroids)
        width = gathered.shape[1]
        local_pts = gathered.shape[0]
        local_cen = centroids.shape[0]
        n_pts = sizes["y"] * sizes["c"]
        n_cen = sizes["x"] * sizes["z"]
        balance = local_pts * n_pts / (local_cen * n_cen)
        row_scale = jnp.ones((local_pts,), jnp.float32)
        col_scale = jnp.ones((local_cen,), jnp.float32)
        scores = jnp.dot(unit_points, unit_centroids.T, preferred_element_type=jnp.float32)
        kernel = jnp.exp(scores / (width * temper))
        for sweep in range(ITERS):
            col_part = jnp.sum(kernel * row_scale[:, None], axis=0)
            col_scale = balance / multi_sum(col_part, pts_red)
            row_part = jnp.sum(kernel * col_scale[None, :], axis=1)
            row_scale = 1.0 / group_sum(row_part, CEN_AXES, n_cen)
        scaled = kernel * row_scale[:, None]
        hi_wide = lax.reduce_precision(scaled, exponent_bits=8, mantissa_bits=7)
        hi = hi_wide.astype(jnp.bfloat16)
        lo = (scaled - hi_wide).astype(jnp.bfloat16)
        mass_part = jnp.sum(scaled, axis=0) * col_scale / balance
        moved = scatter_product(gathered, hi, lo, col_scale, sizes).T
        squares = jnp.sum(moved * moved, axis=1)
        both = multi_sum(jnp.stack([squares, mass_part]), pts_red)
        squares, masses = both[0], both[1]
        new_centroids = moved * lax.rsqrt(squares / width + 1e-06)[:, None]
        return (new_centroids, masses)

    return local


def solution(mesh):
    pts_n, cen_n = mesh.shape["pts"], mesh.shape["cen"]
    cores = 2 if pts_n % 2 == 0 else 1
    zs = 4 if cen_n % 4 == 0 else 1
    sizes = {"y": pts_n // cores, "c": cores, "x": cen_n // zs, "z": zs}
    mesh4 = Mesh(
        mesh.devices.reshape(sizes["y"], sizes["c"], sizes["x"], sizes["z"]),
        ("y", "c", "x", "z"),
    )
    in_specs = (P(PTS_AXES, CEN_AXES), P(CEN_AXES, None))
    out_specs = (P(CEN_AXES, PTS_AXES), P(CEN_AXES))
    return jax.shard_map(
        make_local(sizes), mesh=mesh4, in_specs=in_specs, out_specs=out_specs, check_vma=False
    )
```

```python
import jax
import jax.numpy as jnp
from jax import lax
from jax.experimental import pallas as pl
from jax.sharding import Mesh
from jax.sharding import PartitionSpec as P

ITERS = 3


temper = 0.05

PTS_AXES = ("y", "c")
CEN_AXES = ("x", "z")


def unit_rows(values):
    wide = values.astype(jnp.float32)
    return (wide * lax.rsqrt(jnp.mean(wide * wide, axis=1, keepdims=True) + 1e-06)).astype(
        jnp.bfloat16
    )


def axis_sum(v, axis, n):
    if n == 1:
        return v
    got = [v] + [
        lax.ppermute(v, axis, [(i, (i + s) % n) for i in range(n)]) for s in range(1, n)
    ]
    if n == 2:
        return got[0] + got[1]
    if n == 4:
        return (got[0] + got[2]) + (got[1] + got[3])
    idx = lax.axis_index(axis)
    canon = jnp.stack(got)[(idx - jnp.arange(n)) % n]
    total = canon[0]
    for j in range(1, n):
        total = total + canon[j]
    return total


def group_sum(v, axes, n):
    if n == 1:
        return v
    got = lax.all_to_all(jnp.broadcast_to(v[None], (n,) + v.shape), axes, 0, 0, tiled=False)
    total = got[0]
    for j in range(1, n):
        total = total + got[j]
    return total


def multi_sum(v, axes):
    for axis, n in axes:
        v = axis_sum(v, axis, n)
    return v


def weighted_sum(weights, point_rows):
    return lax.dot_general(
        weights,
        point_rows.astype(jnp.float32),
        (((0,), (0,)), ((), ())),
        precision=lax.Precision.HIGHEST,
        preferred_element_type=jnp.float32,
    )


def scatter_features(part_t, sizes):
    ny, nc = sizes["y"], sizes["c"]
    width, rows = part_t.shape
    blk = width // (ny * nc)
    x = part_t.reshape(ny, nc, blk, rows)
    if nc == 2:
        c = lax.axis_index("c")
        keep = lax.dynamic_index_in_dim(x, c, 1, keepdims=False)
        send = lax.dynamic_index_in_dim(x, 1 - c, 1, keepdims=False)
        x = keep + lax.ppermute(send, "c", [(0, 1), (1, 0)])
    else:
        x = x[:, 0]
    if ny == 1:
        return x[0]
    got = lax.all_to_all(x, "y", 0, 0, tiled=False)
    total = got[0]
    for j in range(1, ny):
        total = total + got[j]
    return total


def ring_gather(v, axis, n):
    if n == 1:
        return v[None]
    if n != 4:
        return lax.all_to_all(jnp.broadcast_to(v[None], (n,) + v.shape), axis, 0, 0, tiled=False)
    fwd = lax.ppermute(v, axis, [(i, (i + 1) % n) for i in range(n)])
    bwd = lax.ppermute(v, axis, [(i, (i - 1) % n) for i in range(n)])
    half = v.shape[-2] // 2
    far = jnp.concatenate(
        [
            lax.ppermute(fwd[..., :half, :], axis, [(i, (i + 1) % n) for i in range(n)]),
            lax.ppermute(bwd[..., half:, :], axis, [(i, (i - 1) % n) for i in range(n)]),
        ],
        axis=-2,
    )
    by_offset = jnp.stack([v, fwd, far, bwd])
    idx = lax.axis_index(axis)
    return by_offset[(idx - jnp.arange(n)) % n]


def gather_features(points, sizes):
    nx, nz = sizes["x"], sizes["z"]
    rows, blk = points.shape
    if nx * nz == 1:
        return points
    if blk % 2 or rows % 2:
        got = lax.all_to_all(
            jnp.broadcast_to(points[None], (nx * nz, rows, blk)), CEN_AXES, 0, 0, tiled=False
        )
        return jnp.transpose(got, (1, 0, 2)).reshape(rows, nx * nz * blk)
    part_a, part_b = points[:, : blk // 2], points[:, blk // 2 :]
    a_z = ring_gather(part_a, "z", nz)
    b_x = ring_gather(part_b, "x", nx)
    a_xz = ring_gather(a_z, "x", nx)
    b_zx = ring_gather(b_x, "z", nz)
    full = jnp.concatenate([a_xz, jnp.transpose(b_zx, (1, 0, 2, 3))], axis=-1)
    return jnp.transpose(full, (2, 0, 1, 3)).reshape(rows, nx * nz * blk)


BLOCK_ROWS = 256


def weighted_col_sums(kernel, row_scale):
    n, m = kernel.shape
    bn = BLOCK_ROWS if n % BLOCK_ROWS == 0 else n

    def body(k_ref, r_ref, o_ref):
        @pl.when(pl.program_id(0) == 0)
        def _():
            o_ref[...] = jnp.zeros_like(o_ref)

        o_ref[...] += jnp.sum(k_ref[...] * r_ref[...], axis=0, keepdims=True)

    out = pl.pallas_call(
        body,
        grid=(n // bn,),
        in_specs=[
            pl.BlockSpec((bn, m), lambda i: (i, 0)),
            pl.BlockSpec((bn, 1), lambda i: (i, 0)),
        ],
        out_specs=pl.BlockSpec((1, m), lambda i: (0, 0)),
        out_shape=jax.ShapeDtypeStruct((1, m), jnp.float32),
        cost_estimate=pl.CostEstimate(flops=2 * n * m, bytes_accessed=4 * n * m, transcendentals=0),
    )(kernel, row_scale[:, None])
    return out[0]


def weighted_row_sums(kernel, col_scale):
    n, m = kernel.shape
    bn = BLOCK_ROWS if n % BLOCK_ROWS == 0 else n

    def body(k_ref, c_ref, o_ref):
        o_ref[...] = jnp.sum(k_ref[...] * c_ref[...], axis=1, keepdims=True)

    out = pl.pallas_call(
        body,
        grid=(n // bn,),
        in_specs=[
            pl.BlockSpec((bn, m), lambda i: (i, 0)),
            pl.BlockSpec((1, m), lambda i: (0, 0)),
        ],
        out_specs=pl.BlockSpec((bn, 1), lambda i: (i, 0)),
        out_shape=jax.ShapeDtypeStruct((n, 1), jnp.float32),
        cost_estimate=pl.CostEstimate(flops=2 * n * m, bytes_accessed=4 * n * m, transcendentals=0),
    )(kernel, col_scale[None, :])
    return out[:, 0]


def make_local(sizes):
    pts_red = [("c", sizes["c"]), ("y", sizes["y"])]
    cen_red = [("z", sizes["z"]), ("x", sizes["x"])]

    def local(points, centroids):
        gathered = gather_features(points, sizes)
        unit_points = unit_rows(gathered)
        unit_centroids = unit_rows(centroids)
        width = gathered.shape[1]
        local_pts = gathered.shape[0]
        local_cen = centroids.shape[0]
        n_pts = sizes["y"] * sizes["c"]
        n_cen = sizes["x"] * sizes["z"]
        balance = local_pts * n_pts / (local_cen * n_cen)
        row_scale = jnp.ones((local_pts,), jnp.float32)
        col_scale = jnp.ones((local_cen,), jnp.float32)
        scores = jnp.dot(unit_points, unit_centroids.T, preferred_element_type=jnp.float32)
        kernel = jnp.exp(scores / (width * temper))
        for sweep in range(ITERS):
            if sweep == 0:
                col_part = jnp.sum(kernel, axis=0)
            else:
                col_part = weighted_col_sums(kernel, row_scale)
            col_scale = balance / multi_sum(col_part, pts_red)
            row_part = weighted_row_sums(kernel, col_scale)
            row_scale = 1.0 / group_sum(row_part, CEN_AXES, n_cen)
        scaled = kernel * row_scale[:, None]
        hi_wide = lax.reduce_precision(scaled, exponent_bits=8, mantissa_bits=7)
        hi = hi_wide.astype(jnp.bfloat16)
        lo = (scaled - hi_wide).astype(jnp.bfloat16)
        dims = (((0,), (0,)), ((), ()))
        partial_t = lax.dot_general(
            gathered, hi, dims, preferred_element_type=jnp.float32
        ) + lax.dot_general(gathered, lo, dims, preferred_element_type=jnp.float32)
        partial_t = partial_t * col_scale[None, :]
        mass_part = jnp.sum(scaled, axis=0) * col_scale / balance
        moved = scatter_features(partial_t, sizes).T
        squares = jnp.sum(moved * moved, axis=1)
        both = multi_sum(jnp.stack([squares, mass_part]), pts_red)
        squares, masses = both[0], both[1]
        new_centroids = moved * lax.rsqrt(squares / width + 1e-06)[:, None]
        return (new_centroids, masses)

    return local


def solution(mesh):
    pts_n, cen_n = mesh.shape["pts"], mesh.shape["cen"]
    cores = 2 if pts_n % 2 == 0 else 1
    zs = 4 if cen_n % 4 == 0 else 1
    sizes = {"y": pts_n // cores, "c": cores, "x": cen_n // zs, "z": zs}
    mesh4 = Mesh(
        mesh.devices.reshape(sizes["y"], sizes["c"], sizes["x"], sizes["z"]),
        ("y", "c", "x", "z"),
    )
    in_specs = (P(PTS_AXES, CEN_AXES), P(CEN_AXES, None))
    out_specs = (P(CEN_AXES, PTS_AXES), P(CEN_AXES))
    return jax.shard_map(
        make_local(sizes), mesh=mesh4, in_specs=in_specs, out_specs=out_specs, check_vma=False
    )
```

```python
import jax
import jax.numpy as jnp
from jax import lax
from jax.sharding import Mesh
from jax.sharding import PartitionSpec as P

ITERS = 3


temper = 0.05

PTS_AXES = ("y", "c")
CEN_AXES = ("x", "z")


def unit_rows(values):
    wide = values.astype(jnp.float32)
    return (wide * lax.rsqrt(jnp.mean(wide * wide, axis=1, keepdims=True) + 1e-06)).astype(
        jnp.bfloat16
    )


def axis_sum(v, axis, n):
    if n == 1:
        return v
    got = [v] + [
        lax.ppermute(v, axis, [(i, (i + s) % n) for i in range(n)]) for s in range(1, n)
    ]
    if n == 2:
        return got[0] + got[1]
    if n == 4:
        return (got[0] + got[2]) + (got[1] + got[3])
    idx = lax.axis_index(axis)
    canon = jnp.stack(got)[(idx - jnp.arange(n)) % n]
    total = canon[0]
    for j in range(1, n):
        total = total + canon[j]
    return total


def group_sum(v, axes, n):
    if n == 1:
        return v
    got = lax.all_to_all(jnp.broadcast_to(v[None], (n,) + v.shape), axes, 0, 0, tiled=False)
    total = got[0]
    for j in range(1, n):
        total = total + got[j]
    return total


def multi_sum(v, axes):
    for axis, n in axes:
        v = axis_sum(v, axis, n)
    return v


def weighted_sum(weights, point_rows):
    return lax.dot_general(
        weights,
        point_rows.astype(jnp.float32),
        (((0,), (0,)), ((), ())),
        precision=lax.Precision.HIGHEST,
        preferred_element_type=jnp.float32,
    )


def scatter_features(part_t, sizes):
    ny, nc = sizes["y"], sizes["c"]
    width, rows = part_t.shape
    blk = width // (ny * nc)
    x = part_t.reshape(ny, nc, blk, rows)
    if nc == 2:
        c = lax.axis_index("c")
        keep = lax.dynamic_index_in_dim(x, c, 1, keepdims=False)
        send = lax.dynamic_index_in_dim(x, 1 - c, 1, keepdims=False)
        x = keep + lax.ppermute(send, "c", [(0, 1), (1, 0)])
    else:
        x = x[:, 0]
    if ny == 1:
        return x[0]
    got = lax.all_to_all(x, "y", 0, 0, tiled=False)
    total = got[0]
    for j in range(1, ny):
        total = total + got[j]
    return total


def ring_gather(v, axis, n):
    if n == 1:
        return v[None]
    if n != 4:
        return lax.all_to_all(jnp.broadcast_to(v[None], (n,) + v.shape), axis, 0, 0, tiled=False)
    fwd = lax.ppermute(v, axis, [(i, (i + 1) % n) for i in range(n)])
    bwd = lax.ppermute(v, axis, [(i, (i - 1) % n) for i in range(n)])
    half = v.shape[-2] // 2
    far = jnp.concatenate(
        [
            lax.ppermute(fwd[..., :half, :], axis, [(i, (i + 1) % n) for i in range(n)]),
            lax.ppermute(bwd[..., half:, :], axis, [(i, (i - 1) % n) for i in range(n)]),
        ],
        axis=-2,
    )
    by_offset = jnp.stack([v, fwd, far, bwd])
    idx = lax.axis_index(axis)
    return by_offset[(idx - jnp.arange(n)) % n]


def gather_features(points, sizes):
    nx, nz = sizes["x"], sizes["z"]
    rows, blk = points.shape
    if nx * nz == 1:
        return points
    if blk % 2 or rows % 2:
        got = lax.all_to_all(
            jnp.broadcast_to(points[None], (nx * nz, rows, blk)), CEN_AXES, 0, 0, tiled=False
        )
        return jnp.transpose(got, (1, 0, 2)).reshape(rows, nx * nz * blk)
    part_a, part_b = points[:, : blk // 2], points[:, blk // 2 :]
    a_z = lax.all_to_all(jnp.broadcast_to(part_a[None], (nz,) + part_a.shape), "z", 0, 0, tiled=False)
    b_x = lax.all_to_all(jnp.broadcast_to(part_b[None], (nx,) + part_b.shape), "x", 0, 0, tiled=False)
    a_xz = ring_gather(a_z, "x", nx)
    b_zx = ring_gather(b_x, "z", nz)
    full = jnp.concatenate([a_xz, jnp.transpose(b_zx, (1, 0, 2, 3))], axis=-1)
    return jnp.transpose(full, (2, 0, 1, 3)).reshape(rows, nx * nz * blk)


def make_local(sizes):
    pts_red = [("c", sizes["c"]), ("y", sizes["y"])]
    cen_red = [("z", sizes["z"]), ("x", sizes["x"])]

    def local(points, centroids):
        gathered = gather_features(points, sizes)
        unit_points = unit_rows(gathered)
        unit_centroids = unit_rows(centroids)
        width = gathered.shape[1]
        local_pts = gathered.shape[0]
        local_cen = centroids.shape[0]
        n_pts = sizes["y"] * sizes["c"]
        n_cen = sizes["x"] * sizes["z"]
        balance = local_pts * n_pts / (local_cen * n_cen)
        row_scale = jnp.ones((local_pts,), jnp.float32)
        col_scale = jnp.ones((local_cen,), jnp.float32)
        scores = jnp.dot(unit_points, unit_centroids.T, preferred_element_type=jnp.float32)
        kernel = jnp.exp(scores / (width * temper))
        for sweep in range(ITERS):
            col_part = jnp.sum(kernel * row_scale[:, None], axis=0)
            col_scale = balance / multi_sum(col_part, pts_red)
            row_part = jnp.sum(kernel * col_scale[None, :], axis=1)
            row_scale = 1.0 / group_sum(row_part, CEN_AXES, n_cen)
        scaled = kernel * row_scale[:, None]
        hi_wide = lax.reduce_precision(scaled, exponent_bits=8, mantissa_bits=7)
        hi = hi_wide.astype(jnp.bfloat16)
        lo = (scaled - hi_wide).astype(jnp.bfloat16)
        dims = (((0,), (0,)), ((), ()))
        partial_t = lax.dot_general(
            gathered, hi, dims, preferred_element_type=jnp.float32
        ) + lax.dot_general(gathered, lo, dims, preferred_element_type=jnp.float32)
        partial_t = partial_t * col_scale[None, :]
        mass_part = jnp.sum(scaled, axis=0) * col_scale / balance
        moved = scatter_features(partial_t, sizes).T
        squares = jnp.sum(moved * moved, axis=1)
        both = multi_sum(jnp.stack([squares, mass_part]), pts_red)
        squares, masses = both[0], both[1]
        new_centroids = moved * lax.rsqrt(squares / width + 1e-06)[:, None]
        return (new_centroids, masses)

    return local


def solution(mesh):
    pts_n, cen_n = mesh.shape["pts"], mesh.shape["cen"]
    cores = 2 if pts_n % 2 == 0 else 1
    zs = 4 if cen_n % 4 == 0 else 1
    sizes = {"y": pts_n // cores, "c": cores, "x": cen_n // zs, "z": zs}
    mesh4 = Mesh(
        mesh.devices.reshape(sizes["y"], sizes["c"], sizes["x"], sizes["z"]),
        ("y", "c", "x", "z"),
    )
    in_specs = (P(PTS_AXES, CEN_AXES), P(CEN_AXES, None))
    out_specs = (P(CEN_AXES, PTS_AXES), P(CEN_AXES))
    return jax.shard_map(
        make_local(sizes), mesh=mesh4, in_specs=in_specs, out_specs=out_specs, check_vma=False
    )
```

```python
import jax
import jax.numpy as jnp
from jax import lax
from jax.sharding import Mesh
from jax.sharding import PartitionSpec as P

ITERS = 3


temper = 0.05

PTS_AXES = ("y", "c")
CEN_AXES = ("x", "z")


def unit_rows(values):
    wide = values.astype(jnp.float32)
    return (wide * lax.rsqrt(jnp.mean(wide * wide, axis=1, keepdims=True) + 1e-06)).astype(
        jnp.bfloat16
    )


def axis_sum(v, axis, n):
    if n == 1:
        return v
    got = [v] + [
        lax.ppermute(v, axis, [(i, (i + s) % n) for i in range(n)]) for s in range(1, n)
    ]
    if n == 2:
        return got[0] + got[1]
    if n == 4:
        return (got[0] + got[2]) + (got[1] + got[3])
    idx = lax.axis_index(axis)
    canon = jnp.stack(got)[(idx - jnp.arange(n)) % n]
    total = canon[0]
    for j in range(1, n):
        total = total + canon[j]
    return total


def group_sum(v, axes, n):
    if n == 1:
        return v
    got = lax.all_to_all(jnp.broadcast_to(v[None], (n,) + v.shape), axes, 0, 0, tiled=False)
    total = got[0]
    for j in range(1, n):
        total = total + got[j]
    return total


def multi_sum(v, axes):
    for axis, n in axes:
        v = axis_sum(v, axis, n)
    return v


def weighted_sum(weights, point_rows):
    return lax.dot_general(
        weights,
        point_rows.astype(jnp.float32),
        (((0,), (0,)), ((), ())),
        precision=lax.Precision.HIGHEST,
        preferred_element_type=jnp.float32,
    )


def scatter_features(part_t, sizes):
    ny, nc = sizes["y"], sizes["c"]
    width, rows = part_t.shape
    blk = width // (ny * nc)
    x = part_t.reshape(ny, nc, blk, rows)
    if nc == 2:
        c = lax.axis_index("c")
        keep = lax.dynamic_index_in_dim(x, c, 1, keepdims=False)
        send = lax.dynamic_index_in_dim(x, 1 - c, 1, keepdims=False)
        x = keep + lax.ppermute(send, "c", [(0, 1), (1, 0)])
    else:
        x = x[:, 0]
    if ny == 1:
        return x[0]
    if ny != 4 or rows % 2:
        got = lax.all_to_all(x, "y", 0, 0, tiled=False)
        total = got[0]
        for j in range(1, ny):
            total = total + got[j]
        return total
    return ring_reduce_scatter(x, "y", ny)


def ring_reduce_scatter(x, axis, n):
    idx = lax.axis_index(axis)
    half = x.shape[-1] // 2
    up, down = x[..., :half], x[..., half:]
    right = [(i, (i + 1) % n) for i in range(n)]
    left = [(i, (i - 1) % n) for i in range(n)]

    def own(part, block):
        return lax.dynamic_index_in_dim(part, block % n, 0, keepdims=False)

    acc_up = own(up, idx + n - 1)
    acc_down = own(down, idx + 1)
    for t in range(1, n):
        recv_up = lax.ppermute(acc_up, axis, right)
        recv_down = lax.ppermute(acc_down, axis, left)
        if t < n - 1:
            acc_up = own(up, idx + n - 1 - t) + recv_up
            acc_down = own(down, idx + 1 + t) + recv_down
        else:
            acc_up = own(up, idx) + recv_up
            acc_down = own(down, idx) + recv_down
    return jnp.concatenate([acc_up, acc_down], axis=-1)


def ring_gather(v, axis, n):
    if n == 1:
        return v[None]
    if n != 4:
        return lax.all_to_all(jnp.broadcast_to(v[None], (n,) + v.shape), axis, 0, 0, tiled=False)
    fwd = lax.ppermute(v, axis, [(i, (i + 1) % n) for i in range(n)])
    bwd = lax.ppermute(v, axis, [(i, (i - 1) % n) for i in range(n)])
    half = v.shape[-2] // 2
    far = jnp.concatenate(
        [
            lax.ppermute(fwd[..., :half, :], axis, [(i, (i + 1) % n) for i in range(n)]),
            lax.ppermute(bwd[..., half:, :], axis, [(i, (i - 1) % n) for i in range(n)]),
        ],
        axis=-2,
    )
    by_offset = jnp.stack([v, fwd, far, bwd])
    idx = lax.axis_index(axis)
    return by_offset[(idx - jnp.arange(n)) % n]


def gather_features(points, sizes):
    nx, nz = sizes["x"], sizes["z"]
    rows, blk = points.shape
    if nx * nz == 1:
        return points
    if blk % 2 or rows % 2:
        got = lax.all_to_all(
            jnp.broadcast_to(points[None], (nx * nz, rows, blk)), CEN_AXES, 0, 0, tiled=False
        )
        return jnp.transpose(got, (1, 0, 2)).reshape(rows, nx * nz * blk)
    part_a, part_b = points[:, : blk // 2], points[:, blk // 2 :]
    a_z = ring_gather(part_a, "z", nz)
    b_x = ring_gather(part_b, "x", nx)
    a_xz = ring_gather(a_z, "x", nx)
    b_zx = ring_gather(b_x, "z", nz)
    full = jnp.concatenate([a_xz, jnp.transpose(b_zx, (1, 0, 2, 3))], axis=-1)
    return jnp.transpose(full, (2, 0, 1, 3)).reshape(rows, nx * nz * blk)


def make_local(sizes):
    pts_red = [("c", sizes["c"]), ("y", sizes["y"])]
    cen_red = [("z", sizes["z"]), ("x", sizes["x"])]

    def local(points, centroids):
        gathered = gather_features(points, sizes)
        unit_points = unit_rows(gathered)
        unit_centroids = unit_rows(centroids)
        width = gathered.shape[1]
        local_pts = gathered.shape[0]
        local_cen = centroids.shape[0]
        n_pts = sizes["y"] * sizes["c"]
        n_cen = sizes["x"] * sizes["z"]
        balance = local_pts * n_pts / (local_cen * n_cen)
        row_scale = jnp.ones((local_pts,), jnp.float32)
        col_scale = jnp.ones((local_cen,), jnp.float32)
        scores = jnp.dot(unit_points, unit_centroids.T, preferred_element_type=jnp.float32)
        kernel = jnp.exp(scores / (width * temper))
        for sweep in range(ITERS):
            col_part = jnp.sum(kernel * row_scale[:, None], axis=0)
            col_scale = balance / multi_sum(col_part, pts_red)
            row_part = jnp.sum(kernel * col_scale[None, :], axis=1)
            row_scale = 1.0 / group_sum(row_part, CEN_AXES, n_cen)
        scaled = kernel * row_scale[:, None]
        hi_wide = lax.reduce_precision(scaled, exponent_bits=8, mantissa_bits=7)
        hi = hi_wide.astype(jnp.bfloat16)
        lo = (scaled - hi_wide).astype(jnp.bfloat16)
        dims = (((0,), (0,)), ((), ()))
        partial_t = lax.dot_general(
            gathered, hi, dims, preferred_element_type=jnp.float32
        ) + lax.dot_general(gathered, lo, dims, preferred_element_type=jnp.float32)
        partial_t = partial_t * col_scale[None, :]
        mass_part = jnp.sum(scaled, axis=0) * col_scale / balance
        moved = scatter_features(partial_t, sizes).T
        squares = jnp.sum(moved * moved, axis=1)
        both = multi_sum(jnp.stack([squares, mass_part]), pts_red)
        squares, masses = both[0], both[1]
        new_centroids = moved * lax.rsqrt(squares / width + 1e-06)[:, None]
        return (new_centroids, masses)

    return local


def solution(mesh):
    pts_n, cen_n = mesh.shape["pts"], mesh.shape["cen"]
    cores = 2 if pts_n % 2 == 0 else 1
    zs = 4 if cen_n % 4 == 0 else 1
    sizes = {"y": pts_n // cores, "c": cores, "x": cen_n // zs, "z": zs}
    mesh4 = Mesh(
        mesh.devices.reshape(sizes["y"], sizes["c"], sizes["x"], sizes["z"]),
        ("y", "c", "x", "z"),
    )
    in_specs = (P(PTS_AXES, CEN_AXES), P(CEN_AXES, None))
    out_specs = (P(CEN_AXES, PTS_AXES), P(CEN_AXES))
    return jax.shard_map(
        make_local(sizes), mesh=mesh4, in_specs=in_specs, out_specs=out_specs, check_vma=False
    )
```

```python
import jax
import jax.numpy as jnp
from jax import lax
from jax.sharding import Mesh
from jax.sharding import PartitionSpec as P

ITERS = 3


temper = 0.05

PTS_AXES = ("y", "c")
CEN_AXES = ("x", "z")


def unit_rows(values):
    wide = values.astype(jnp.float32)
    return (wide * lax.rsqrt(jnp.mean(wide * wide, axis=1, keepdims=True) + 1e-06)).astype(
        jnp.bfloat16
    )


def axis_sum(v, axis, n):
    if n == 1:
        return v
    got = [v] + [
        lax.ppermute(v, axis, [(i, (i + s) % n) for i in range(n)]) for s in range(1, n)
    ]
    if n == 2:
        return got[0] + got[1]
    if n == 4:
        return (got[0] + got[2]) + (got[1] + got[3])
    idx = lax.axis_index(axis)
    canon = jnp.stack(got)[(idx - jnp.arange(n)) % n]
    total = canon[0]
    for j in range(1, n):
        total = total + canon[j]
    return total


def group_sum(v, axes, n):
    if n == 1:
        return v
    got = lax.all_to_all(jnp.broadcast_to(v[None], (n,) + v.shape), axes, 0, 0, tiled=False)
    total = got[0]
    for j in range(1, n):
        total = total + got[j]
    return total


def multi_sum(v, axes):
    for axis, n in axes:
        v = axis_sum(v, axis, n)
    return v


def weighted_sum(weights, point_rows):
    return lax.dot_general(
        weights,
        point_rows.astype(jnp.float32),
        (((0,), (0,)), ((), ())),
        precision=lax.Precision.HIGHEST,
        preferred_element_type=jnp.float32,
    )


def scatter_features(part_t, sizes):
    ny, nc = sizes["y"], sizes["c"]
    width, rows = part_t.shape
    blk = width // (ny * nc)
    x = part_t.reshape(ny, nc, blk, rows)
    if nc == 2:
        c = lax.axis_index("c")
        keep = lax.dynamic_index_in_dim(x, c, 1, keepdims=False)
        send = lax.dynamic_index_in_dim(x, 1 - c, 1, keepdims=False)
        x = keep + lax.ppermute(send, "c", [(0, 1), (1, 0)])
    else:
        x = x[:, 0]
    if ny == 1:
        return x[0]
    got = lax.all_to_all(x, "y", 0, 0, tiled=False)
    total = got[0]
    for j in range(1, ny):
        total = total + got[j]
    return total


def ring_gather(v, axis, n, split_far=True):
    if n == 1:
        return v[None]
    if n != 4:
        return lax.all_to_all(jnp.broadcast_to(v[None], (n,) + v.shape), axis, 0, 0, tiled=False)
    fwd = lax.ppermute(v, axis, [(i, (i + 1) % n) for i in range(n)])
    bwd = lax.ppermute(v, axis, [(i, (i - 1) % n) for i in range(n)])
    half = v.shape[-2] // 2
    if split_far:
        far = jnp.concatenate(
            [
                lax.ppermute(fwd[..., :half, :], axis, [(i, (i + 1) % n) for i in range(n)]),
                lax.ppermute(bwd[..., half:, :], axis, [(i, (i - 1) % n) for i in range(n)]),
            ],
            axis=-2,
        )
    else:
        far = lax.ppermute(fwd, axis, [(i, (i + 1) % n) for i in range(n)])
    by_offset = jnp.stack([v, fwd, far, bwd])
    idx = lax.axis_index(axis)
    return by_offset[(idx - jnp.arange(n)) % n]


def gather_features(points, sizes):
    nx, nz = sizes["x"], sizes["z"]
    rows, blk = points.shape
    if nx * nz == 1:
        return points
    if blk % 2 or rows % 2:
        got = lax.all_to_all(
            jnp.broadcast_to(points[None], (nx * nz, rows, blk)), CEN_AXES, 0, 0, tiled=False
        )
        return jnp.transpose(got, (1, 0, 2)).reshape(rows, nx * nz * blk)
    part_a, part_b = points[:, : blk // 2], points[:, blk // 2 :]
    a_z = ring_gather(part_a, "z", nz, split_far=False)
    b_x = ring_gather(part_b, "x", nx, split_far=False)
    a_xz = ring_gather(a_z, "x", nx)
    b_zx = ring_gather(b_x, "z", nz)
    full = jnp.concatenate([a_xz, jnp.transpose(b_zx, (1, 0, 2, 3))], axis=-1)
    return jnp.transpose(full, (2, 0, 1, 3)).reshape(rows, nx * nz * blk)


def make_local(sizes):
    pts_red = [("c", sizes["c"]), ("y", sizes["y"])]
    cen_red = [("z", sizes["z"]), ("x", sizes["x"])]

    def local(points, centroids):
        gathered = gather_features(points, sizes)
        unit_points = unit_rows(gathered)
        unit_centroids = unit_rows(centroids)
        width = gathered.shape[1]
        local_pts = gathered.shape[0]
        local_cen = centroids.shape[0]
        n_pts = sizes["y"] * sizes["c"]
        n_cen = sizes["x"] * sizes["z"]
        balance = local_pts * n_pts / (local_cen * n_cen)
        row_scale = jnp.ones((local_pts,), jnp.float32)
        col_scale = jnp.ones((local_cen,), jnp.float32)
        scores = jnp.dot(unit_points, unit_centroids.T, preferred_element_type=jnp.float32)
        kernel = jnp.exp(scores / (width * temper))
        for sweep in range(ITERS):
            col_part = jnp.sum(kernel * row_scale[:, None], axis=0)
            col_scale = balance / multi_sum(col_part, pts_red)
            row_part = jnp.sum(kernel * col_scale[None, :], axis=1)
            row_scale = 1.0 / group_sum(row_part, CEN_AXES, n_cen)
        scaled = kernel * row_scale[:, None]
        hi_wide = lax.reduce_precision(scaled, exponent_bits=8, mantissa_bits=7)
        hi = hi_wide.astype(jnp.bfloat16)
        lo = (scaled - hi_wide).astype(jnp.bfloat16)
        dims = (((0,), (0,)), ((), ()))
        partial_t = lax.dot_general(
            gathered, hi, dims, preferred_element_type=jnp.float32
        ) + lax.dot_general(gathered, lo, dims, preferred_element_type=jnp.float32)
        partial_t = partial_t * col_scale[None, :]
        mass_part = jnp.sum(scaled, axis=0) * col_scale / balance
        moved = scatter_features(partial_t, sizes).T
        squares = jnp.sum(moved * moved, axis=1)
        both = multi_sum(jnp.stack([squares, mass_part]), pts_red)
        squares, masses = both[0], both[1]
        new_centroids = moved * lax.rsqrt(squares / width + 1e-06)[:, None]
        return (new_centroids, masses)

    return local


def solution(mesh):
    pts_n, cen_n = mesh.shape["pts"], mesh.shape["cen"]
    cores = 2 if pts_n % 2 == 0 else 1
    zs = 4 if cen_n % 4 == 0 else 1
    sizes = {"y": pts_n // cores, "c": cores, "x": cen_n // zs, "z": zs}
    mesh4 = Mesh(
        mesh.devices.reshape(sizes["y"], sizes["c"], sizes["x"], sizes["z"]),
        ("y", "c", "x", "z"),
    )
    in_specs = (P(PTS_AXES, CEN_AXES), P(CEN_AXES, None))
    out_specs = (P(CEN_AXES, PTS_AXES), P(CEN_AXES))
    return jax.shard_map(
        make_local(sizes), mesh=mesh4, in_specs=in_specs, out_specs=out_specs, check_vma=False
    )
```

```python
import jax
import jax.numpy as jnp
from jax import lax
from jax.sharding import Mesh
from jax.sharding import PartitionSpec as P

ITERS = 3


temper = 0.05

PTS_AXES = ("y", "c")
CEN_AXES = ("x", "z")


def unit_rows(values):
    wide = values.astype(jnp.float32)
    return (wide * lax.rsqrt(jnp.mean(wide * wide, axis=1, keepdims=True) + 1e-06)).astype(
        jnp.bfloat16
    )


def axis_sum(v, axis, n):
    if n == 1:
        return v
    got = [v] + [
        lax.ppermute(v, axis, [(i, (i + s) % n) for i in range(n)]) for s in range(1, n)
    ]
    if n == 2:
        return got[0] + got[1]
    if n == 4:
        return (got[0] + got[2]) + (got[1] + got[3])
    idx = lax.axis_index(axis)
    canon = jnp.stack(got)[(idx - jnp.arange(n)) % n]
    total = canon[0]
    for j in range(1, n):
        total = total + canon[j]
    return total


def group_sum(v, axes, n):
    if n == 1:
        return v
    got = lax.all_to_all(jnp.broadcast_to(v[None], (n,) + v.shape), axes, 0, 0, tiled=False)
    total = got[0]
    for j in range(1, n):
        total = total + got[j]
    return total


def multi_sum(v, axes):
    for axis, n in axes:
        v = axis_sum(v, axis, n)
    return v


def weighted_sum(weights, point_rows):
    return lax.dot_general(
        weights,
        point_rows.astype(jnp.float32),
        (((0,), (0,)), ((), ())),
        precision=lax.Precision.HIGHEST,
        preferred_element_type=jnp.float32,
    )


def own_first(point_rows, sizes):
    ny, nc = sizes["y"], sizes["c"]
    rows, width = point_rows.shape
    if nc != 2:
        return point_rows
    blk = width // (ny * nc)
    split = point_rows.reshape(rows, ny, nc, blk)
    c = lax.axis_index("c")
    keep = lax.dynamic_index_in_dim(split, c, 2, keepdims=False)
    send = lax.dynamic_index_in_dim(split, 1 - c, 2, keepdims=False)
    return jnp.stack([keep, send], axis=1).reshape(rows, width)


def scatter_features(part_t, sizes):
    ny, nc = sizes["y"], sizes["c"]
    width, rows = part_t.shape
    blk = width // (ny * nc)
    if nc == 2:
        keep, send = part_t[: width // 2], part_t[width // 2 :]
        x = keep + lax.ppermute(send, "c", [(0, 1), (1, 0)])
    else:
        x = part_t
    x = x.reshape(ny, blk, rows)
    if ny == 1:
        return x[0]
    got = lax.all_to_all(x, "y", 0, 0, tiled=False)
    total = got[0]
    for j in range(1, ny):
        total = total + got[j]
    return total


def ring_gather(v, axis, n, split_far=True):
    if n == 1:
        return v[None]
    if n != 4:
        return lax.all_to_all(jnp.broadcast_to(v[None], (n,) + v.shape), axis, 0, 0, tiled=False)
    fwd = lax.ppermute(v, axis, [(i, (i + 1) % n) for i in range(n)])
    bwd = lax.ppermute(v, axis, [(i, (i - 1) % n) for i in range(n)])
    half = v.shape[-2] // 2
    if split_far:
        far = jnp.concatenate(
            [
                lax.ppermute(fwd[..., :half, :], axis, [(i, (i + 1) % n) for i in range(n)]),
                lax.ppermute(bwd[..., half:, :], axis, [(i, (i - 1) % n) for i in range(n)]),
            ],
            axis=-2,
        )
    else:
        far = lax.ppermute(fwd, axis, [(i, (i + 1) % n) for i in range(n)])
    by_offset = jnp.stack([v, fwd, far, bwd])
    idx = lax.axis_index(axis)
    return by_offset[(idx - jnp.arange(n)) % n]


def gather_features(points, sizes):
    nx, nz = sizes["x"], sizes["z"]
    rows, blk = points.shape
    if nx * nz == 1:
        return points
    if blk % 2 or rows % 2:
        got = lax.all_to_all(
            jnp.broadcast_to(points[None], (nx * nz, rows, blk)), CEN_AXES, 0, 0, tiled=False
        )
        return jnp.transpose(got, (1, 0, 2)).reshape(rows, nx * nz * blk)
    part_a, part_b = points[:, : blk // 2], points[:, blk // 2 :]
    a_z = ring_gather(part_a, "z", nz, split_far=False)
    b_x = ring_gather(part_b, "x", nx, split_far=False)
    a_xz = ring_gather(a_z, "x", nx)
    b_zx = ring_gather(b_x, "z", nz)
    full = jnp.concatenate([a_xz, jnp.transpose(b_zx, (1, 0, 2, 3))], axis=-1)
    return jnp.transpose(full, (2, 0, 1, 3)).reshape(rows, nx * nz * blk)


def make_local(sizes):
    pts_red = [("c", sizes["c"]), ("y", sizes["y"])]
    cen_red = [("z", sizes["z"]), ("x", sizes["x"])]

    def local(points, centroids):
        gathered = gather_features(points, sizes)
        unit_points = unit_rows(gathered)
        unit_centroids = unit_rows(centroids)
        width = gathered.shape[1]
        local_pts = gathered.shape[0]
        local_cen = centroids.shape[0]
        n_pts = sizes["y"] * sizes["c"]
        n_cen = sizes["x"] * sizes["z"]
        balance = local_pts * n_pts / (local_cen * n_cen)
        row_scale = jnp.ones((local_pts,), jnp.float32)
        col_scale = jnp.ones((local_cen,), jnp.float32)
        scores = jnp.dot(unit_points, unit_centroids.T, preferred_element_type=jnp.float32)
        kernel = jnp.exp(scores / (width * temper))
        for sweep in range(ITERS):
            col_part = jnp.sum(kernel * row_scale[:, None], axis=0)
            col_scale = balance / multi_sum(col_part, pts_red)
            row_part = jnp.sum(kernel * col_scale[None, :], axis=1)
            row_scale = 1.0 / group_sum(row_part, CEN_AXES, n_cen)
        scaled = kernel * row_scale[:, None]
        hi_wide = lax.reduce_precision(scaled, exponent_bits=8, mantissa_bits=7)
        hi = hi_wide.astype(jnp.bfloat16)
        lo = (scaled - hi_wide).astype(jnp.bfloat16)
        dims = (((0,), (0,)), ((), ()))
        ordered = own_first(gathered, sizes)
        partial_t = lax.dot_general(
            ordered, hi, dims, preferred_element_type=jnp.float32
        ) + lax.dot_general(ordered, lo, dims, preferred_element_type=jnp.float32)
        partial_t = partial_t * col_scale[None, :]
        mass_part = jnp.sum(scaled, axis=0) * col_scale / balance
        moved = scatter_features(partial_t, sizes).T
        squares = jnp.sum(moved * moved, axis=1)
        both = multi_sum(jnp.stack([squares, mass_part]), pts_red)
        squares, masses = both[0], both[1]
        new_centroids = moved * lax.rsqrt(squares / width + 1e-06)[:, None]
        return (new_centroids, masses)

    return local


def solution(mesh):
    pts_n, cen_n = mesh.shape["pts"], mesh.shape["cen"]
    cores = 2 if pts_n % 2 == 0 else 1
    zs = 4 if cen_n % 4 == 0 else 1
    sizes = {"y": pts_n // cores, "c": cores, "x": cen_n // zs, "z": zs}
    mesh4 = Mesh(
        mesh.devices.reshape(sizes["y"], sizes["c"], sizes["x"], sizes["z"]),
        ("y", "c", "x", "z"),
    )
    in_specs = (P(PTS_AXES, CEN_AXES), P(CEN_AXES, None))
    out_specs = (P(CEN_AXES, PTS_AXES), P(CEN_AXES))
    return jax.shard_map(
        make_local(sizes), mesh=mesh4, in_specs=in_specs, out_specs=out_specs, check_vma=False
    )
```

```python
import jax
import jax.numpy as jnp
from jax import lax
from jax.sharding import Mesh
from jax.sharding import PartitionSpec as P

ITERS = 3


temper = 0.05

PTS_AXES = ("y", "c")
CEN_AXES = ("x", "z")


def unit_rows(values):
    wide = values.astype(jnp.float32)
    return (wide * lax.rsqrt(jnp.mean(wide * wide, axis=1, keepdims=True) + 1e-06)).astype(
        jnp.bfloat16
    )


def axis_sum(v, axis, n):
    if n == 1:
        return v
    got = [v] + [
        lax.ppermute(v, axis, [(i, (i + s) % n) for i in range(n)]) for s in range(1, n)
    ]
    if n == 2:
        return got[0] + got[1]
    if n == 4:
        return (got[0] + got[2]) + (got[1] + got[3])
    idx = lax.axis_index(axis)
    canon = jnp.stack(got)[(idx - jnp.arange(n)) % n]
    total = canon[0]
    for j in range(1, n):
        total = total + canon[j]
    return total


def group_sum(v, axes, n):
    if n == 1:
        return v
    got = lax.all_to_all(jnp.broadcast_to(v[None], (n,) + v.shape), axes, 0, 0, tiled=False)
    total = got[0]
    for j in range(1, n):
        total = total + got[j]
    return total


def multi_sum(v, axes):
    for axis, n in axes:
        v = axis_sum(v, axis, n)
    return v


def weighted_sum(weights, point_rows):
    return lax.dot_general(
        weights,
        point_rows.astype(jnp.float32),
        (((0,), (0,)), ((), ())),
        precision=lax.Precision.HIGHEST,
        preferred_element_type=jnp.float32,
    )


def scatter_features(part_t, sizes):
    ny, nc = sizes["y"], sizes["c"]
    width, rows = part_t.shape
    blk = width // (ny * nc)
    x = part_t.reshape(ny, nc, blk, rows)
    if nc == 2:
        c = lax.axis_index("c")
        keep = lax.dynamic_index_in_dim(x, c, 1, keepdims=False)
        send = lax.dynamic_index_in_dim(x, 1 - c, 1, keepdims=False)
        x = keep + lax.ppermute(send, "c", [(0, 1), (1, 0)])
    else:
        x = x[:, 0]
    if ny == 1:
        return x[0]
    got = lax.all_to_all(x, "y", 0, 0, tiled=False)
    total = got[0]
    for j in range(1, ny):
        total = total + got[j]
    return total


def ring_gather(v, axis, n, split_far=True):
    if n == 1:
        return v[None]
    if n != 4:
        return lax.all_to_all(jnp.broadcast_to(v[None], (n,) + v.shape), axis, 0, 0, tiled=False)
    fwd = lax.ppermute(v, axis, [(i, (i + 1) % n) for i in range(n)])
    bwd = lax.ppermute(v, axis, [(i, (i - 1) % n) for i in range(n)])
    half = v.shape[-2] // 2
    if split_far:
        far = jnp.concatenate(
            [
                lax.ppermute(fwd[..., :half, :], axis, [(i, (i + 1) % n) for i in range(n)]),
                lax.ppermute(bwd[..., half:, :], axis, [(i, (i - 1) % n) for i in range(n)]),
            ],
            axis=-2,
        )
    else:
        far = lax.ppermute(fwd, axis, [(i, (i + 1) % n) for i in range(n)])
    by_offset = jnp.stack([v, fwd, far, bwd])
    idx = lax.axis_index(axis)
    return by_offset[(idx - jnp.arange(n)) % n]


def gather_features(points, sizes):
    nx, nz = sizes["x"], sizes["z"]
    rows, blk = points.shape
    if nx * nz == 1:
        return points
    if blk % 2 or rows % 2:
        got = lax.all_to_all(
            jnp.broadcast_to(points[None], (nx * nz, rows, blk)), CEN_AXES, 0, 0, tiled=False
        )
        return jnp.transpose(got, (1, 0, 2)).reshape(rows, nx * nz * blk)
    part_a, part_b = points[:, : blk // 2], points[:, blk // 2 :]
    a_z = ring_gather(part_a, "z", nz, split_far=False)
    b_x = ring_gather(part_b, "x", nx, split_far=False)
    a_xz = ring_gather(a_z, "x", nx, split_far=False)
    b_zx = ring_gather(b_x, "z", nz, split_far=False)
    full = jnp.concatenate([a_xz, jnp.transpose(b_zx, (1, 0, 2, 3))], axis=-1)
    return jnp.transpose(full, (2, 0, 1, 3)).reshape(rows, nx * nz * blk)


def make_local(sizes):
    pts_red = [("c", sizes["c"]), ("y", sizes["y"])]
    cen_red = [("z", sizes["z"]), ("x", sizes["x"])]

    def local(points, centroids):
        gathered = gather_features(points, sizes)
        unit_points = unit_rows(gathered)
        unit_centroids = unit_rows(centroids)
        width = gathered.shape[1]
        local_pts = gathered.shape[0]
        local_cen = centroids.shape[0]
        n_pts = sizes["y"] * sizes["c"]
        n_cen = sizes["x"] * sizes["z"]
        balance = local_pts * n_pts / (local_cen * n_cen)
        row_scale = jnp.ones((local_pts,), jnp.float32)
        col_scale = jnp.ones((local_cen,), jnp.float32)
        scores = jnp.dot(unit_points, unit_centroids.T, preferred_element_type=jnp.float32)
        kernel = jnp.exp(scores / (width * temper))
        for sweep in range(ITERS):
            col_part = jnp.sum(kernel * row_scale[:, None], axis=0)
            col_scale = balance / multi_sum(col_part, pts_red)
            row_part = jnp.sum(kernel * col_scale[None, :], axis=1)
            row_scale = 1.0 / group_sum(row_part, CEN_AXES, n_cen)
        scaled = kernel * row_scale[:, None]
        hi_wide = lax.reduce_precision(scaled, exponent_bits=8, mantissa_bits=7)
        hi = hi_wide.astype(jnp.bfloat16)
        lo = (scaled - hi_wide).astype(jnp.bfloat16)
        dims = (((0,), (0,)), ((), ()))
        partial_t = lax.dot_general(
            gathered, hi, dims, preferred_element_type=jnp.float32
        ) + lax.dot_general(gathered, lo, dims, preferred_element_type=jnp.float32)
        partial_t = partial_t * col_scale[None, :]
        mass_part = jnp.sum(scaled, axis=0) * col_scale / balance
        moved = scatter_features(partial_t, sizes).T
        squares = jnp.sum(moved * moved, axis=1)
        both = multi_sum(jnp.stack([squares, mass_part]), pts_red)
        squares, masses = both[0], both[1]
        new_centroids = moved * lax.rsqrt(squares / width + 1e-06)[:, None]
        return (new_centroids, masses)

    return local


def solution(mesh):
    pts_n, cen_n = mesh.shape["pts"], mesh.shape["cen"]
    cores = 2 if pts_n % 2 == 0 else 1
    zs = 4 if cen_n % 4 == 0 else 1
    sizes = {"y": pts_n // cores, "c": cores, "x": cen_n // zs, "z": zs}
    mesh4 = Mesh(
        mesh.devices.reshape(sizes["y"], sizes["c"], sizes["x"], sizes["z"]),
        ("y", "c", "x", "z"),
    )
    in_specs = (P(PTS_AXES, CEN_AXES), P(CEN_AXES, None))
    out_specs = (P(CEN_AXES, PTS_AXES), P(CEN_AXES))
    return jax.shard_map(
        make_local(sizes), mesh=mesh4, in_specs=in_specs, out_specs=out_specs, check_vma=False
    )
```

```python
import jax
import jax.numpy as jnp
from jax import lax
from jax.sharding import Mesh
from jax.sharding import PartitionSpec as P

ITERS = 3


temper = 0.05

PTS_AXES = ("y", "c")
CEN_AXES = ("x", "z")


def unit_rows(values):
    wide = values.astype(jnp.float32)
    return (wide * lax.rsqrt(jnp.mean(wide * wide, axis=1, keepdims=True) + 1e-06)).astype(
        jnp.bfloat16
    )


def axis_sum(v, axis, n):
    if n == 1:
        return v
    got = [v] + [
        lax.ppermute(v, axis, [(i, (i + s) % n) for i in range(n)]) for s in range(1, n)
    ]
    if n == 2:
        return got[0] + got[1]
    if n == 4:
        return (got[0] + got[2]) + (got[1] + got[3])
    idx = lax.axis_index(axis)
    canon = jnp.stack(got)[(idx - jnp.arange(n)) % n]
    total = canon[0]
    for j in range(1, n):
        total = total + canon[j]
    return total


def group_sum(v, axes, n):
    if n == 1:
        return v
    got = lax.all_to_all(jnp.broadcast_to(v[None], (n,) + v.shape), axes, 0, 0, tiled=False)
    total = got[0]
    for j in range(1, n):
        total = total + got[j]
    return total


def multi_sum(v, axes):
    for axis, n in axes:
        v = axis_sum(v, axis, n)
    return v


def weighted_sum(weights, point_rows):
    return lax.dot_general(
        weights,
        point_rows.astype(jnp.float32),
        (((0,), (0,)), ((), ())),
        precision=lax.Precision.HIGHEST,
        preferred_element_type=jnp.float32,
    )


def scatter_features(part_t, sizes):
    ny, nc = sizes["y"], sizes["c"]
    width, rows = part_t.shape
    blk = width // (ny * nc)
    x = part_t.reshape(ny, nc, blk, rows)
    if nc == 2:
        c = lax.axis_index("c")
        keep = lax.dynamic_index_in_dim(x, c, 1, keepdims=False)
        send = lax.dynamic_index_in_dim(x, 1 - c, 1, keepdims=False)
        x = keep + lax.ppermute(send, "c", [(0, 1), (1, 0)])
    else:
        x = x[:, 0]
    if ny == 1:
        return x[0]
    got = lax.all_to_all(x, "y", 0, 0, tiled=False)
    total = got[0]
    for j in range(1, ny):
        total = total + got[j]
    return total


def ring_gather(v, axis, n, split_far=True):
    if n == 1:
        return v[None]
    if n != 4:
        return lax.all_to_all(jnp.broadcast_to(v[None], (n,) + v.shape), axis, 0, 0, tiled=False)
    fwd = lax.ppermute(v, axis, [(i, (i + 1) % n) for i in range(n)])
    bwd = lax.ppermute(v, axis, [(i, (i - 1) % n) for i in range(n)])
    half = v.shape[-2] // 2
    if split_far:
        far = jnp.concatenate(
            [
                lax.ppermute(fwd[..., :half, :], axis, [(i, (i + 1) % n) for i in range(n)]),
                lax.ppermute(bwd[..., half:, :], axis, [(i, (i - 1) % n) for i in range(n)]),
            ],
            axis=-2,
        )
    else:
        far = lax.ppermute(fwd, axis, [(i, (i + 1) % n) for i in range(n)])
    by_offset = jnp.stack([v, fwd, far, bwd])
    idx = lax.axis_index(axis)
    return by_offset[(idx - jnp.arange(n)) % n]


def gather_features(points, sizes):
    nx, nz = sizes["x"], sizes["z"]
    rows, blk = points.shape
    if nx * nz == 1:
        return points
    if blk % 2 or rows % 2:
        got = lax.all_to_all(
            jnp.broadcast_to(points[None], (nx * nz, rows, blk)), CEN_AXES, 0, 0, tiled=False
        )
        return jnp.transpose(got, (1, 0, 2)).reshape(rows, nx * nz * blk)
    part_a, part_b = points[:, : blk // 2], points[:, blk // 2 :]
    a_z = ring_gather(part_a, "z", nz, split_far=False)
    b_x = ring_gather(part_b, "x", nx, split_far=False)
    a_xz = ring_gather(a_z, "x", nx, split_far=False)
    b_zx = ring_gather(b_x, "z", nz, split_far=False)
    full = jnp.concatenate([a_xz, jnp.transpose(b_zx, (1, 0, 2, 3))], axis=-1)
    return jnp.transpose(full, (2, 0, 1, 3)).reshape(rows, nx * nz * blk)


def make_local(sizes):
    pts_red = [("c", sizes["c"]), ("y", sizes["y"])]
    cen_red = [("z", sizes["z"]), ("x", sizes["x"])]

    def local(points, centroids):
        gathered = gather_features(points, sizes)
        unit_points = unit_rows(gathered)
        unit_centroids = unit_rows(centroids)
        width = gathered.shape[1]
        local_pts = gathered.shape[0]
        local_cen = centroids.shape[0]
        n_pts = sizes["y"] * sizes["c"]
        n_cen = sizes["x"] * sizes["z"]
        balance = local_pts * n_pts / (local_cen * n_cen)
        row_scale = jnp.ones((local_pts,), jnp.float32)
        col_scale = jnp.ones((local_cen,), jnp.float32)
        scores = jnp.dot(unit_points, unit_centroids.T, preferred_element_type=jnp.float32)
        kernel = jnp.exp(scores / (width * temper))
        for sweep in range(ITERS):
            col_part = jnp.sum(kernel * row_scale[:, None], axis=0)
            col_scale = balance / group_sum(col_part, PTS_AXES, n_pts)
            row_part = jnp.sum(kernel * col_scale[None, :], axis=1)
            row_scale = 1.0 / group_sum(row_part, CEN_AXES, n_cen)
        scaled = kernel * row_scale[:, None]
        hi_wide = lax.reduce_precision(scaled, exponent_bits=8, mantissa_bits=7)
        hi = hi_wide.astype(jnp.bfloat16)
        lo = (scaled - hi_wide).astype(jnp.bfloat16)
        dims = (((0,), (0,)), ((), ()))
        partial_t = lax.dot_general(
            gathered, hi, dims, preferred_element_type=jnp.float32
        ) + lax.dot_general(gathered, lo, dims, preferred_element_type=jnp.float32)
        partial_t = partial_t * col_scale[None, :]
        mass_part = jnp.sum(scaled, axis=0) * col_scale / balance
        moved = scatter_features(partial_t, sizes).T
        squares = jnp.sum(moved * moved, axis=1)
        both = group_sum(jnp.stack([squares, mass_part]), PTS_AXES, n_pts)
        squares, masses = both[0], both[1]
        new_centroids = moved * lax.rsqrt(squares / width + 1e-06)[:, None]
        return (new_centroids, masses)

    return local


def solution(mesh):
    pts_n, cen_n = mesh.shape["pts"], mesh.shape["cen"]
    cores = 2 if pts_n % 2 == 0 else 1
    zs = 4 if cen_n % 4 == 0 else 1
    sizes = {"y": pts_n // cores, "c": cores, "x": cen_n // zs, "z": zs}
    mesh4 = Mesh(
        mesh.devices.reshape(sizes["y"], sizes["c"], sizes["x"], sizes["z"]),
        ("y", "c", "x", "z"),
    )
    in_specs = (P(PTS_AXES, CEN_AXES), P(CEN_AXES, None))
    out_specs = (P(CEN_AXES, PTS_AXES), P(CEN_AXES))
    return jax.shard_map(
        make_local(sizes), mesh=mesh4, in_specs=in_specs, out_specs=out_specs, check_vma=False
    )
```

```python
import jax
import jax.numpy as jnp
from jax import lax
from jax.sharding import Mesh
from jax.sharding import PartitionSpec as P

ITERS = 3


temper = 0.05

PTS_AXES = ("y", "c")
CEN_AXES = ("x", "z")


def unit_rows(values):
    wide = values.astype(jnp.float32)
    return (wide * lax.rsqrt(jnp.mean(wide * wide, axis=1, keepdims=True) + 1e-06)).astype(
        jnp.bfloat16
    )


def axis_sum(v, axis, n):
    if n == 1:
        return v
    got = [v] + [
        lax.ppermute(v, axis, [(i, (i + s) % n) for i in range(n)]) for s in range(1, n)
    ]
    if n == 2:
        return got[0] + got[1]
    if n == 4:
        return (got[0] + got[2]) + (got[1] + got[3])
    idx = lax.axis_index(axis)
    canon = jnp.stack(got)[(idx - jnp.arange(n)) % n]
    total = canon[0]
    for j in range(1, n):
        total = total + canon[j]
    return total


def group_sum(v, axes, n):
    if n == 1:
        return v
    got = lax.all_to_all(jnp.broadcast_to(v[None], (n,) + v.shape), axes, 0, 0, tiled=False)
    total = got[0]
    for j in range(1, n):
        total = total + got[j]
    return total


def multi_sum(v, axes):
    for axis, n in axes:
        v = axis_sum(v, axis, n)
    return v


def weighted_sum(weights, point_rows):
    return lax.dot_general(
        weights,
        point_rows.astype(jnp.float32),
        (((0,), (0,)), ((), ())),
        precision=lax.Precision.HIGHEST,
        preferred_element_type=jnp.float32,
    )


def scatter_features(part_t, sizes):
    ny, nc = sizes["y"], sizes["c"]
    width, rows = part_t.shape
    blk = width // (ny * nc)
    x = part_t.reshape(ny, nc, blk, rows)
    if nc == 2:
        c = lax.axis_index("c")
        keep = lax.dynamic_index_in_dim(x, c, 1, keepdims=False)
        send = lax.dynamic_index_in_dim(x, 1 - c, 1, keepdims=False)
        x = keep + lax.ppermute(send, "c", [(0, 1), (1, 0)])
    else:
        x = x[:, 0]
    if ny == 1:
        return x[0]
    got = lax.all_to_all(x, "y", 0, 0, tiled=False)
    total = got[0]
    for j in range(1, ny):
        total = total + got[j]
    return total


def ring_gather(v, axis, n, split_far=True, reorder=True):
    if n == 1:
        return v[None]
    if n != 4:
        return lax.all_to_all(jnp.broadcast_to(v[None], (n,) + v.shape), axis, 0, 0, tiled=False)
    fwd = lax.ppermute(v, axis, [(i, (i + 1) % n) for i in range(n)])
    bwd = lax.ppermute(v, axis, [(i, (i - 1) % n) for i in range(n)])
    half = v.shape[-2] // 2
    if split_far:
        far = jnp.concatenate(
            [
                lax.ppermute(fwd[..., :half, :], axis, [(i, (i + 1) % n) for i in range(n)]),
                lax.ppermute(bwd[..., half:, :], axis, [(i, (i - 1) % n) for i in range(n)]),
            ],
            axis=-2,
        )
    else:
        far = lax.ppermute(fwd, axis, [(i, (i + 1) % n) for i in range(n)])
    by_offset = jnp.stack([v, fwd, far, bwd])
    if not reorder:
        return by_offset
    idx = lax.axis_index(axis)
    return by_offset[(idx - jnp.arange(n)) % n]


def gather_features(points, sizes):
    nx, nz = sizes["x"], sizes["z"]
    rows, blk = points.shape
    if nx * nz == 1:
        return points
    if blk % 2 or rows % 2:
        got = lax.all_to_all(
            jnp.broadcast_to(points[None], (nx * nz, rows, blk)), CEN_AXES, 0, 0, tiled=False
        )
        return jnp.transpose(got, (1, 0, 2)).reshape(rows, nx * nz * blk)
    part_a, part_b = points[:, : blk // 2], points[:, blk // 2 :]
    if nx != 4 or nz != 4:
        a_xz = ring_gather(ring_gather(part_a, "z", nz, split_far=False), "x", nx, split_far=False)
        b_zx = ring_gather(ring_gather(part_b, "x", nx, split_far=False), "z", nz, split_far=False)
    else:
        ix, iz = lax.axis_index("x"), lax.axis_index("z")
        a_off = ring_gather(
            ring_gather(part_a, "z", nz, split_far=False, reorder=False),
            "x", nx, split_far=False, reorder=False,
        )
        b_off = ring_gather(
            ring_gather(part_b, "x", nx, split_far=False, reorder=False),
            "z", nz, split_far=False, reorder=False,
        )
        ox = (ix - jnp.arange(nx)) % nx
        oz = (iz - jnp.arange(nz)) % nz
        a_sel = (ox[:, None] * nz + oz[None, :]).reshape(-1)
        b_sel = (oz[:, None] * nx + ox[None, :]).reshape(-1)
        a_xz = a_off.reshape((nx * nz,) + a_off.shape[2:])[a_sel].reshape(a_off.shape)
        b_zx = b_off.reshape((nx * nz,) + b_off.shape[2:])[b_sel].reshape(b_off.shape)
    full = jnp.concatenate([a_xz, jnp.transpose(b_zx, (1, 0, 2, 3))], axis=-1)
    return jnp.transpose(full, (2, 0, 1, 3)).reshape(rows, nx * nz * blk)


def make_local(sizes):
    pts_red = [("c", sizes["c"]), ("y", sizes["y"])]
    cen_red = [("z", sizes["z"]), ("x", sizes["x"])]

    def local(points, centroids):
        gathered = gather_features(points, sizes)
        unit_points = unit_rows(gathered)
        unit_centroids = unit_rows(centroids)
        width = gathered.shape[1]
        local_pts = gathered.shape[0]
        local_cen = centroids.shape[0]
        n_pts = sizes["y"] * sizes["c"]
        n_cen = sizes["x"] * sizes["z"]
        balance = local_pts * n_pts / (local_cen * n_cen)
        row_scale = jnp.ones((local_pts,), jnp.float32)
        col_scale = jnp.ones((local_cen,), jnp.float32)
        scores = jnp.dot(unit_points, unit_centroids.T, preferred_element_type=jnp.float32)
        kernel = jnp.exp(scores / (width * temper))
        for sweep in range(ITERS):
            col_part = jnp.sum(kernel * row_scale[:, None], axis=0)
            col_scale = balance / multi_sum(col_part, pts_red)
            row_part = jnp.sum(kernel * col_scale[None, :], axis=1)
            row_scale = 1.0 / group_sum(row_part, CEN_AXES, n_cen)
        scaled = kernel * row_scale[:, None]
        hi_wide = lax.reduce_precision(scaled, exponent_bits=8, mantissa_bits=7)
        hi = hi_wide.astype(jnp.bfloat16)
        lo = (scaled - hi_wide).astype(jnp.bfloat16)
        dims = (((0,), (0,)), ((), ()))
        partial_t = lax.dot_general(
            gathered, hi, dims, preferred_element_type=jnp.float32
        ) + lax.dot_general(gathered, lo, dims, preferred_element_type=jnp.float32)
        partial_t = partial_t * col_scale[None, :]
        mass_part = jnp.sum(scaled, axis=0) * col_scale / balance
        moved = scatter_features(partial_t, sizes).T
        squares = jnp.sum(moved * moved, axis=1)
        both = multi_sum(jnp.stack([squares, mass_part]), pts_red)
        squares, masses = both[0], both[1]
        new_centroids = moved * lax.rsqrt(squares / width + 1e-06)[:, None]
        return (new_centroids, masses)

    return local


def solution(mesh):
    pts_n, cen_n = mesh.shape["pts"], mesh.shape["cen"]
    cores = 2 if pts_n % 2 == 0 else 1
    zs = 4 if cen_n % 4 == 0 else 1
    sizes = {"y": pts_n // cores, "c": cores, "x": cen_n // zs, "z": zs}
    mesh4 = Mesh(
        mesh.devices.reshape(sizes["y"], sizes["c"], sizes["x"], sizes["z"]),
        ("y", "c", "x", "z"),
    )
    in_specs = (P(PTS_AXES, CEN_AXES), P(CEN_AXES, None))
    out_specs = (P(CEN_AXES, PTS_AXES), P(CEN_AXES))
    return jax.shard_map(
        make_local(sizes), mesh=mesh4, in_specs=in_specs, out_specs=out_specs, check_vma=False
    )
```
